128 devices in a mesh: req: 4 (over z), blk: 32 (over y, x, core).
Axes of the slice: x: 4, y: 4, z: 4, core: 2. Of those that a mesh axis runs over, the one named last changes fastest.
Arguments:
- queries: bfloat16 [4, 2048, 2048], P('req', 'blk'), may hold values from -6 to 6
- span_keys: bfloat16 [4, 2048, 512], P('req', 'blk'), may hold values from -6 to 6
- span_values: bfloat16 [4, 2048, 512], P('req', 'blk'), may hold values from -6 to 6
- cache_keys: bfloat16 [4, 4096, 512], P('req', 'blk'), may hold values from -6 to 6
- cache_values: bfloat16 [4, 4096, 512], P('req', 'blk'), may hold values from -6 to 6
- lengths: int32 [4], P('req'), may hold values from 1 to 4096, 10240 in all
- inputs: bfloat16 [4, 2048, 2048], P('req', 'blk'), may hold values from -0.59765625 to 0.59765625
- w_out: bfloat16 [2048, 2048], replicated, may hold values from -0.125 to 0.125
- norm_gain: float32 [2048], replicated, may hold values from 0.1 to 1.9
- route_ids: int32 [4, 2048, 6], P('req', 'blk'), may hold values from 0 to 63, all different within a row; in each aligned block of 64 rows (0 to 63, 64 to 127, ..., all dimensions but the last counted through in order) at most 12 rows name the same one
- route_weights: float32 [4, 2048, 6], P('req', 'blk'), may hold values from 0.2 to 1
- w_gate_up: bfloat16 [128, 1408, 2048], P(('req', 'blk')), may hold values from -0.125 to 0.125
- w_down: bfloat16 [128, 704, 2048], P(('req', 'blk')), may hold values from -0.15625 to 0.15625
Outputs:
- outputs: bfloat16 [4, 2048, 2048], P('req', 'blk')
The draws below stay inside these ranges and needn't reach their ends.
Inputs may be any that keep to these rules, and one draw needn't show every extreme that they name: `lengths`: the longest cache is exactly 4096. `route_ids`: A token names 6 different experts; within the rows of one device (aligned blocks of 64 tokens) no expert is named more than 12 times, a bound that some block reaches.
All inputs are finite; a program needn't handle non-finite values. No bound on the sum of `lengths` on one device may be relied on, other than what follows from the above.
Results may differ from the reference program's by a relative error of at most 0.019.
Values may be sent and summed in bfloat16 or wider, within the bound.
No kernel may reach another device: no remote copies, remote signals or barrier semaphores. Data moves between devices by JAX's collectives and lax.ppermute only.
A program may use at most 256 MiB of HBM per device.

```python
import math
import jax
import jax.numpy as jnp
import numpy as np
from jax import lax

D = 2048
HEADS = 16
KV_HEADS = 4
HEAD_DIM = 128
FF_E = 1408
EXPERTS = 64
TOP = 6
SPAN = 2048
CTX = 4096
REQS = 4
TOK_DEV = 64
HALF = 704
CAP = 12
N_BLK = 32


def draw_queries(key, part):
    full_shape = (REQS, SPAN, HEADS * HEAD_DIM)
    return (1.4 * jax.random.truncated_normal(jax.random.fold_in(key, 1), -4.0, 4.0, full_shape, jnp.float32)).astype(jnp.bfloat16)


def draw_span_keys(key, part):
    full_shape = (REQS, SPAN, KV_HEADS * HEAD_DIM)
    return jax.random.truncated_normal(jax.random.fold_in(key, 2), -4.0, 4.0, full_shape, jnp.float32).astype(jnp.bfloat16)


def levels(own_key, extent, shards, least, largest):
    level, own = 1.0, jax.random.fold_in(own_key, 6)
    for position, shards_of in shards:
        steps = jnp.exp(jax.random.uniform(jax.random.fold_in(own, position), (shards_of,), jnp.float32, least / len(shards), largest / len(shards)))
        level = level * jnp.repeat(steps, extent[position] // shards_of).reshape([-1 if axis == position else 1 for axis in range(len(extent))])
    return level


def length_profile(count, total, limit, lean):
    weights = [(1 << 20) // math.isqrt(standing ** lean) + 1 for standing in range(2, count + 1)]
    surplus, counts = total - limit - (count - 1), [1] * (count - 1)
    while surplus > 0:
        free = [i for i in range(count - 1) if counts[i] < limit]
        mass, left = sum([weights[i] for i in free]), surplus
        for i in free:
            extra = min(limit - counts[i], max(1, left * weights[i] // mass), surplus)
            counts[i] = counts[i] + extra
            surplus = surplus - extra
    return np.array([limit] + counts)


def ragged(stream_key, count, total, reach, skew):
    if count == 2:
        one = jax.random.randint(stream_key, (), max(1, total - reach), min(reach, total - 1) + 1)
        return jnp.stack([one, total - one])
    sizes = jnp.asarray(length_profile(count, total, reach, skew), jnp.int32)
    couples = (count - 1) // 2
    donor, taker = sizes[1:1 + 2 * couples:2], sizes[2:2 + 2 * couples:2]
    slack = jnp.minimum(donor - 1, reach - taker)
    shifted = jax.random.randint(jax.random.fold_in(stream_key, 1), (couples,), 0, 1 << 20) % (slack + 1)
    sizes = sizes.at[1:1 + 2 * couples:2].set(donor - shifted).at[2:2 + 2 * couples:2].set(taker + shifted)
    return sizes[jax.random.permutation(jax.random.fold_in(stream_key, 2), count)]


def routed_block(key, own, number, rows, amount, top, limit, slope):
    sequence = jax.random.permutation(key, amount)
    crowded, usual = shares(amount, rows * top, limit, slope, True), shares(amount, rows * top, limit, slope, False)
    places = jnp.arange(amount)

    def named(sizes, turn):
        used = int((sizes > 0).sum())
        fixed = max(1, used // 4)
        shifted = fixed + (places - fixed + turn * (used - fixed)) % max(1, amount - fixed)
        return jnp.zeros((amount,), jnp.int32).at[sequence[jnp.where(places < fixed, places, shifted)]].set(jnp.asarray(sizes, jnp.int32))

    sizes = jnp.where(number % 4 == 0, named(crowded, number // 4), named(usual, number - number // 4 - 1))
    mixed = jax.random.permutation(jax.random.fold_in(own, 3), amount)
    giver, sink = mixed[0:amount // 2 * 2:2], mixed[1:amount // 2 * 2:2]
    margin = jnp.minimum(sizes[giver] - 1, limit - sizes[sink]) // 2
    margin = jnp.where((giver == sequence[0]) | (sink == sequence[0]) | (sizes[sink] == 0), 0, jnp.maximum(margin, 0))
    shifted = jax.random.randint(jax.random.fold_in(own, 4), (amount // 2,), 0, 1 << 20) % (margin + 1)
    sizes = sizes.at[giver].add(-shifted).at[sink].add(shifted)
    items = jnp.searchsorted(jnp.cumsum(sizes), jnp.arange(rows * top), side="right").astype(jnp.int32)
    table = items.reshape(top, rows).T
    table = table[jax.random.permutation(jax.random.fold_in(own, 1), rows)]
    turn = jax.random.randint(jax.random.fold_in(own, 2), (rows, 1), 0, top)
    return jnp.take_along_axis(table, (jnp.arange(top)[None, :] + turn) % top, axis=1)


def shares(number_of, total, bound, lean, full):
    loads = [(1 << 20) // math.isqrt(standing ** lean) + 1 for standing in range(1, number_of + 1)]
    largest = bound if full else min(bound, max(-(-total // number_of), total * loads[0] // sum(loads)))
    least = 1 if total - largest >= number_of - 1 else 0
    given, rest = [largest] + [least] * (number_of - 1), total - largest - least * (number_of - 1)
    while rest > 0:
        free = [i for i in range(1, number_of) if given[i] < largest] or [i for i in range(1, number_of) if given[i] < bound]
        mass, remaining = sum([loads[i] for i in free]), rest
        for i in free:
            more = min(bound - given[i], max(1, remaining * loads[i] // mass), rest)
            given[i] = given[i] + more
            rest = rest - more
    return np.array(given)


def normal_values(key, shape, scale, bound, cuts=(), held_as=jnp.bfloat16):
    drawn = scale * jax.random.normal(key, shape, jnp.float32)
    if cuts:
        drawn = drawn * levels(key, shape, cuts, -0.22, 0.18)
    return jnp.clip(drawn, -bound, bound).astype(held_as)


def setup_inputs(seed: int = 0) -> dict:
    key_of = jax.random.split(jax.random.key(seed), 14)
    queries = draw_queries(jax.random.fold_in(key_of[13], 71), 0)
    span_keys = draw_span_keys(jax.random.fold_in(key_of[13], 71), 0)
    span_values = normal_values(key_of[2], (REQS, SPAN, KV_HEADS * HEAD_DIM), 1.0, 6.0, ((0, 4), (1, 32)))
    cache_keys = normal_values(key_of[3], (REQS, CTX, KV_HEADS * HEAD_DIM), 1.0, 6.0, ((0, 4), (1, 32)))
    cache_values = normal_values(key_of[4], (REQS, CTX, KV_HEADS * HEAD_DIM), 1.0, 6.0, ((0, 4), (1, 32)))
    lengths = ragged(key_of[5], REQS, 2 * CTX + CTX // 2, CTX, 2).astype(jnp.int32)
    inputs = normal_values(key_of[6], (REQS, SPAN, D), 0.1, 0.59765625, ((0, 4), (1, 32)))
    w_out = normal_values(key_of[7], (HEADS * HEAD_DIM, D), (HEADS * HEAD_DIM) ** -0.5, 0.125)
    norm_gain = jnp.clip(1.0 + 0.18 * jax.random.normal(key_of[8], (D,), jnp.float32), 0.1, 1.9)
    route_ids_keys = jax.random.split(jax.random.fold_in(key_of[9], 1), REQS * SPAN // TOK_DEV)
    route_ids_turns = jax.random.permutation(jax.random.fold_in(key_of[9], 3), REQS * SPAN // TOK_DEV)
    route_ids = jax.vmap(lambda own, number: routed_block(jax.random.fold_in(key_of[9], 2), own, number, TOK_DEV, EXPERTS, TOP, CAP, 2))(route_ids_keys, route_ids_turns).reshape((REQS, SPAN, TOP))
    route_weights = jnp.clip(0.2 + 0.8 * jax.random.uniform(key_of[10], (REQS, SPAN, TOP), jnp.float32) ** levels(key_of[10], (REQS, SPAN, TOP), ((0, 4), (1, 32)), -0.2, 0.2), 0.2, 1.0)
    w_gate_up = normal_values(key_of[11], (2 * EXPERTS, 2 * HALF, D), D ** -0.5, 0.125, ((0, 128),))
    w_down = normal_values(key_of[12], (2 * EXPERTS, HALF, D), FF_E ** -0.5, 0.15625, ((0, 128),))
    return dict(queries=queries, span_keys=span_keys, span_values=span_values, cache_keys=cache_keys, cache_values=cache_values, lengths=lengths, inputs=inputs, w_out=w_out, norm_gain=norm_gain, route_ids=route_ids, route_weights=route_weights, w_gate_up=w_gate_up, w_down=w_down)


def attend_request(query_rows, key_rows, value_rows, length):
    group_size = HEADS // KV_HEADS
    keys_wide = key_rows.astype(jnp.float32).reshape(-1, KV_HEADS, HEAD_DIM)
    values_wide = value_rows.astype(jnp.float32).reshape(-1, KV_HEADS, HEAD_DIM)
    key_index = jnp.arange(key_rows.shape[0], dtype=jnp.int32)
    block_size = min(256, SPAN)
    starts = jnp.arange(SPAN // block_size, dtype=jnp.int32) * block_size

    def one_block(first_row):
        picked = lax.dynamic_slice_in_dim(query_rows, first_row, block_size, 0)
        picked = picked.astype(jnp.float32).reshape(block_size, KV_HEADS, group_size, HEAD_DIM)
        scores = jnp.einsum('qgrd,kgd->qgrk', picked, keys_wide) / math.sqrt(HEAD_DIM)
        row_index = first_row + jnp.arange(block_size, dtype=jnp.int32)
        in_cache = (key_index < CTX) & (key_index < length)
        in_span = (key_index >= CTX) & (key_index - CTX <= row_index[:, None])
        visible = (in_cache[None, :] | in_span)[:, None, None, :]
        masked = jnp.where(visible, scores, -1e+30)
        row_peak = lax.optimization_barrier(jnp.max(masked, axis=-1, keepdims=True))
        probs_now = jnp.where(visible, jnp.exp(masked - row_peak), 0.0)
        row_total = lax.optimization_barrier(jnp.sum(probs_now, axis=-1))
        rounded = lax.optimization_barrier(probs_now.astype(jnp.bfloat16)).astype(jnp.float32)
        mixed_rows = jnp.einsum('qgrk,kgd->qgrd', rounded, values_wide) / row_total[..., None]
        return mixed_rows.reshape(block_size, HEADS * HEAD_DIM).astype(jnp.bfloat16)
    return lax.map(one_block, starts).reshape(SPAN, HEADS * HEAD_DIM)

def reference(queries, span_keys, span_values, cache_keys, cache_values, lengths, inputs, w_out, norm_gain, route_ids, route_weights, w_gate_up, w_down):
    attended = jnp.stack([attend_request(queries[request], jnp.concatenate([cache_keys[request], span_keys[request]], 0), jnp.concatenate([cache_values[request], span_values[request]], 0), lengths[request]) for request in range(REQS)])
    token_count = REQS * SPAN
    residual = inputs.reshape(token_count, D).astype(jnp.float32) + jnp.dot(attended.reshape(token_count, HEADS * HEAD_DIM), w_out, preferred_element_type=jnp.float32)
    normalized = (residual * lax.rsqrt(lax.optimization_barrier(jnp.mean(residual * residual, axis=-1, keepdims=True)) + 1e-06) * norm_gain).astype(jnp.bfloat16)
    tok_dev = SPAN // N_BLK
    blocks = token_count // tok_dev
    expert_ids = route_ids.reshape(blocks, tok_dev * TOP)
    onehot = (expert_ids[..., None] == jnp.arange(EXPERTS, dtype=jnp.int32)).astype(jnp.int32)
    earlier = jnp.cumsum(onehot, axis=1) - onehot
    slot_index = lax.optimization_barrier(jnp.sum(earlier * onehot, axis=-1))
    token_of = (jnp.arange(token_count * TOP, dtype=jnp.int32) // TOP).reshape(blocks, -1)
    block_of = jnp.broadcast_to(jnp.arange(blocks, dtype=jnp.int32)[:, None], expert_ids.shape)
    slot_table = jnp.full((EXPERTS, blocks, CAP), token_count, jnp.int32).at[expert_ids, block_of, slot_index].set(token_of)
    scale_table = jnp.zeros((EXPERTS, blocks, CAP), jnp.float32).at[expert_ids, block_of, slot_index].set(route_weights.reshape(blocks, -1).astype(jnp.float32))
    padded = jnp.concatenate([normalized, jnp.zeros((1, D), jnp.bfloat16)], 0)

    def one_expert(running, expert):
        rows_index = lax.dynamic_index_in_dim(slot_table, expert, 0, keepdims=False).reshape(-1)
        picked = padded[rows_index]
        summed = jnp.zeros((picked.shape[0], D), jnp.float32)
        for half_index in range(2):
            gate_up = lax.dynamic_index_in_dim(w_gate_up, 2 * expert + half_index, 0, keepdims=False)
            hidden = jnp.dot(picked, gate_up.T, preferred_element_type=jnp.float32)
            activated = (jax.nn.silu(hidden[:, :HALF]) * hidden[:, HALF:]).astype(jnp.bfloat16)
            down_rows = lax.dynamic_index_in_dim(w_down, 2 * expert + half_index, 0, keepdims=False)
            partial_value = jnp.dot(activated, down_rows, preferred_element_type=jnp.float32)
            summed = summed + lax.optimization_barrier(partial_value.astype(jnp.bfloat16)).astype(jnp.float32)
        factor = lax.dynamic_index_in_dim(scale_table, expert, 0, keepdims=False).reshape(-1)
        running = running.at[rows_index].add(factor[:, None] * summed, mode='drop')
        return (running, None)
    expert_sum, _ = lax.scan(one_expert, jnp.zeros((token_count, D), jnp.float32), jnp.arange(EXPERTS, dtype=jnp.int32))
    return (residual + expert_sum).astype(jnp.bfloat16).reshape(REQS, SPAN, D)
```

```python
import math

import jax
import jax.numpy as jnp
from jax import lax
from jax.sharding import PartitionSpec as P

D = 2048
HEADS = 16
KV_HEADS = 4
HEAD_DIM = 128
EXPERTS = 64
TOP = 6


def attend(queries, kv_rows, length, blk_index, cache_len, span_len):
    tok_rows = queries.shape[0]
    group_size = HEADS // KV_HEADS
    per_dev = cache_len + span_len
    key_count = kv_rows.shape[0]
    key_rows = kv_rows[:, : KV_HEADS * HEAD_DIM].reshape(key_count, KV_HEADS, HEAD_DIM)
    value_rows = kv_rows[:, KV_HEADS * HEAD_DIM :].reshape(key_count, KV_HEADS, HEAD_DIM)
    key_index = jnp.arange(key_count, dtype=jnp.int32)
    owner = key_index // per_dev
    offset = key_index % per_dev
    in_cache = (offset < cache_len) & (owner * cache_len + offset < length)
    span_pos = owner * span_len + offset - cache_len
    row_index = blk_index * tok_rows + jnp.arange(tok_rows, dtype=jnp.int32)
    in_span = (offset >= cache_len)[None, :] & (span_pos[None, :] <= row_index[:, None])
    visible = (in_cache[None, :] | in_span)[:, None, None, :]
    query_rows = queries.reshape(tok_rows, KV_HEADS, group_size, HEAD_DIM)
    scores = jnp.einsum(
        "qgrd,kgd->qgrk", query_rows, key_rows, preferred_element_type=jnp.float32
    ) / math.sqrt(HEAD_DIM)
    masked = jnp.where(visible, scores, -1e30)
    row_peak = jnp.max(masked, axis=-1, keepdims=True)
    probs = jnp.where(visible, jnp.exp(masked - row_peak), 0.0)
    row_total = jnp.sum(probs, axis=-1)
    weighted = jnp.einsum(
        "qgrk,kgd->qgrd",
        probs.astype(jnp.bfloat16),
        value_rows,
        preferred_element_type=jnp.float32,
    )
    return (weighted / row_total[..., None]).reshape(tok_rows, HEADS * HEAD_DIM).astype(jnp.bfloat16)


def half_expert(arrived, gate_up, down_rows):
    half_width = down_rows.shape[0]
    hidden = jnp.dot(arrived, gate_up.T, preferred_element_type=jnp.float32)
    activated = (jax.nn.silu(hidden[:, :half_width]) * hidden[:, half_width:]).astype(jnp.bfloat16)
    return jnp.dot(activated, down_rows, preferred_element_type=jnp.float32).astype(jnp.bfloat16)


def local(
    queries,
    span_keys,
    span_values,
    cache_keys,
    cache_values,
    lengths,
    inputs,
    w_out,
    norm_gain,
    route_ids,
    route_weights,
    w_gate_up,
    w_down,
):
    tok_rows = queries.shape[1]
    blk_count = lax.axis_size("blk")
    blk_index = lax.axis_index("blk")
    length = lengths[0]
    cache_len = cache_keys.shape[1]
    span_len = span_keys.shape[1]

    pairs = [(b, b ^ 1) for b in range(blk_count)]
    other_gate_up = lax.ppermute(w_gate_up[0], "blk", pairs)
    other_down = lax.ppermute(w_down[0], "blk", pairs)

    local_kv = jnp.concatenate(
        [
            jnp.concatenate([cache_keys[0], span_keys[0]], 0),
            jnp.concatenate([cache_values[0], span_values[0]], 0),
        ],
        1,
    )
    kv_rows = lax.all_gather(local_kv, "blk", axis=0, tiled=True)
    attended = attend(queries[0], kv_rows, length, blk_index, cache_len, span_len)

    residual = inputs[0].astype(jnp.float32) + jnp.dot(
        attended, w_out, preferred_element_type=jnp.float32
    )
    normalized = (
        residual
        * lax.rsqrt(jnp.mean(residual * residual, axis=-1, keepdims=True) + 1e-06)
        * norm_gain
    ).astype(jnp.bfloat16)

    devices = lax.axis_size("req") * blk_count
    capacity = max(2, tok_rows * TOP * 2 // EXPERTS)
    half_cap = (capacity + 1) // 2
    flat_ids = route_ids[0].reshape(-1)
    onehot = (flat_ids[:, None] == jnp.arange(EXPERTS, dtype=jnp.int32)[None, :]).astype(jnp.int32)
    slot_index = jnp.sum((jnp.cumsum(onehot, axis=0) - onehot) * onehot, axis=1)
    slot_target = (2 * flat_ids + slot_index % 2) * half_cap + slot_index // 2
    slot_match = slot_target[:, None] == jnp.arange(devices * half_cap, dtype=jnp.int32)[None, :]
    dispatch = jnp.sum(slot_match.reshape(tok_rows, TOP, -1).astype(jnp.float32), axis=1).astype(
        jnp.bfloat16
    )
    combine_weights = jnp.sum(
        jnp.where(slot_match, route_weights[0].reshape(-1)[:, None], 0.0).reshape(
            tok_rows, TOP, -1
        ),
        axis=1,
    )
    outgoing = lax.dot_general(
        dispatch, normalized, (((0,), (0,)), ((), ())), preferred_element_type=jnp.float32
    ).astype(jnp.bfloat16)
    arrived = lax.all_to_all(
        outgoing.reshape(devices, half_cap, D), ("req", "blk"), split_axis=0, concat_axis=0, tiled=True
    ).reshape(devices * half_cap, D)
    mine = half_expert(arrived, w_gate_up[0], w_down[0])
    other = half_expert(arrived, other_gate_up, other_down)
    both = (mine.astype(jnp.float32) + other.astype(jnp.float32)).astype(jnp.bfloat16)
    returned = lax.all_to_all(
        both.reshape(devices, half_cap, D), ("req", "blk"), split_axis=0, concat_axis=0, tiled=True
    ).reshape(devices * half_cap, D)
    expert_sum = jnp.dot(
        combine_weights,
        returned.astype(jnp.float32),
        precision=lax.Precision.HIGHEST,
        preferred_element_type=jnp.float32,
    )
    return (residual + expert_sum).astype(jnp.bfloat16)[None]


def solution(mesh):
    in_specs = (
        P("req", "blk", None),
        P("req", "blk", None),
        P("req", "blk", None),
        P("req", "blk", None),
        P("req", "blk", None),
        P("req"),
        P("req", "blk", None),
        P(),
        P(),
        P("req", "blk", None),
        P("req", "blk", None),
        P(("req", "blk"), None, None),
        P(("req", "blk"), None, None),
    )
    out_specs = P("req", "blk", None)
    return jax.shard_map(local, mesh=mesh, in_specs=in_specs, out_specs=out_specs, check_vma=False)
```

```python
import math

import jax
import jax.numpy as jnp
from jax import lax
from jax.experimental import pallas as pl
from jax.experimental.pallas import tpu as pltpu
from jax.sharding import PartitionSpec as P

D = 2048
HEADS = 16
KV_HEADS = 4
HEAD_DIM = 128
EXPERTS = 64
TOP = 6


CHUNK = 512


def attn_kernel(s_ref, q_ref, ck_ref, cv_ref, sk_ref, sv_ref, o_ref):
    group_size = HEADS // KV_HEADS
    tok_rows = q_ref.shape[0]
    rows = tok_rows * group_size
    length = s_ref[0]
    blk = s_ref[1]
    qb = q_ref[...]
    qs = jnp.concatenate([qb[:, r * HEAD_DIM:(r + 1) * HEAD_DIM] for r in range(group_size)], axis=0)
    qpos = blk * tok_rows + lax.broadcasted_iota(jnp.int32, (rows, 1), 0) % tok_rows
    col = lax.broadcasted_iota(jnp.int32, (1, CHUNK), 1)
    n_cache = (length + CHUNK - 1) // CHUNK
    n_span = (blk * tok_rows + tok_rows - 1) // CHUNK + 1
    scale = math.sqrt(HEAD_DIM)

    def scores(k_ref, c):
        k = k_ref[pl.ds(pl.multiple_of(c * CHUNK, CHUNK), CHUNK), :]
        return lax.dot_general(qs, k, (((1,), (1,)), ((), ())), preferred_element_type=jnp.float32) / scale

    def cache_mask(c):
        return (c * CHUNK + col) < length

    def span_mask(c):
        return (c * CHUNK + col) <= qpos

    def peak_step(k_ref, mask_of):
        def body(c, m):
            s = jnp.where(mask_of(c), scores(k_ref, c), -1e30)
            return jnp.maximum(m, jnp.max(s, axis=-1, keepdims=True))
        return body

    m = jnp.full((rows, 1), -1e30, jnp.float32)
    m = lax.fori_loop(0, n_cache, peak_step(ck_ref, cache_mask), m)
    m = lax.fori_loop(0, n_span, peak_step(sk_ref, span_mask), m)

    def sum_step(k_ref, v_ref, mask_of):
        def body(c, carry):
            l, acc = carry
            mask = mask_of(c)
            s = jnp.where(mask, scores(k_ref, c), -1e30)
            p = jnp.where(mask, jnp.exp(s - m), 0.0)
            v = v_ref[pl.ds(pl.multiple_of(c * CHUNK, CHUNK), CHUNK), :]
            l = l + jnp.sum(p, axis=-1, keepdims=True)
            acc = acc + jnp.dot(p.astype(jnp.bfloat16), v, preferred_element_type=jnp.float32)
            return l, acc
        return body

    carry = (jnp.zeros((rows, 1), jnp.float32), jnp.zeros((rows, HEAD_DIM), jnp.float32))
    carry = lax.fori_loop(0, n_cache, sum_step(ck_ref, cv_ref, cache_mask), carry)
    l, acc = lax.fori_loop(0, n_span, sum_step(sk_ref, sv_ref, span_mask), carry)
    out = (acc / l).astype(o_ref.dtype)
    for r in range(group_size):
        o_ref[:, r * HEAD_DIM:(r + 1) * HEAD_DIM] = out[r * tok_rows:(r + 1) * tok_rows]


def attention(scalars, queries, cache_kv, span_kv):
    tok_rows = queries.shape[0]
    cache_len = cache_kv.shape[0]
    span_len = span_kv.shape[0]
    group_cols = HEAD_DIM * HEADS // KV_HEADS
    return pl.pallas_call(
        attn_kernel,
        out_shape=jax.ShapeDtypeStruct(queries.shape, jnp.bfloat16),
        grid=(KV_HEADS,),
        in_specs=[
            pl.BlockSpec(memory_space=pltpu.SMEM),
            pl.BlockSpec((tok_rows, group_cols), lambda g: (0, g)),
            pl.BlockSpec((cache_len, HEAD_DIM), lambda g: (0, g)),
            pl.BlockSpec((cache_len, HEAD_DIM), lambda g: (0, KV_HEADS + g)),
            pl.BlockSpec((span_len, HEAD_DIM), lambda g: (0, g)),
            pl.BlockSpec((span_len, HEAD_DIM), lambda g: (0, KV_HEADS + g)),
        ],
        out_specs=pl.BlockSpec((tok_rows, group_cols), lambda g: (0, g)),
        compiler_params=pltpu.CompilerParams(
            dimension_semantics=("arbitrary",), vmem_limit_bytes=40 * 1024 * 1024
        ),
    )(scalars, queries, cache_kv, cache_kv, span_kv, span_kv)


def half_expert(arrived, gate_up, down_rows):
    half_width = down_rows.shape[0]
    hidden = jnp.dot(arrived, gate_up.T, preferred_element_type=jnp.float32)
    activated = (jax.nn.silu(hidden[:, :half_width]) * hidden[:, half_width:]).astype(jnp.bfloat16)
    return jnp.dot(activated, down_rows, preferred_element_type=jnp.float32).astype(jnp.bfloat16)


def local(
    queries,
    span_keys,
    span_values,
    cache_keys,
    cache_values,
    lengths,
    inputs,
    w_out,
    norm_gain,
    route_ids,
    route_weights,
    w_gate_up,
    w_down,
):
    tok_rows = queries.shape[1]
    blk_count = lax.axis_size("blk")
    blk_index = lax.axis_index("blk")
    length = lengths[0]
    cache_len = cache_keys.shape[1]
    span_len = span_keys.shape[1]

    pairs = [(b, b ^ 1) for b in range(blk_count)]
    other_gate_up = lax.ppermute(w_gate_up[0], "blk", pairs)
    other_down = lax.ppermute(w_down[0], "blk", pairs)

    cache_kv, span_kv = lax.all_gather(
        (
            jnp.concatenate([cache_keys[0], cache_values[0]], 1),
            jnp.concatenate([span_keys[0], span_values[0]], 1),
        ),
        "blk",
        axis=0,
        tiled=True,
    )
    scalars = jnp.stack([length, blk_index.astype(jnp.int32)])
    attended = attention(scalars, queries[0], cache_kv, span_kv)

    residual = inputs[0].astype(jnp.float32) + jnp.dot(
        attended, w_out, preferred_element_type=jnp.float32
    )
    normalized = (
        residual
        * lax.rsqrt(jnp.mean(residual * residual, axis=-1, keepdims=True) + 1e-06)
        * norm_gain
    ).astype(jnp.bfloat16)

    devices = lax.axis_size("req") * blk_count
    capacity = max(2, tok_rows * TOP * 2 // EXPERTS)
    half_cap = (capacity + 1) // 2
    flat_ids = route_ids[0].reshape(-1)
    onehot = (flat_ids[:, None] == jnp.arange(EXPERTS, dtype=jnp.int32)[None, :]).astype(jnp.int32)
    slot_index = jnp.sum((jnp.cumsum(onehot, axis=0) - onehot) * onehot, axis=1)
    slot_target = (2 * flat_ids + slot_index % 2) * half_cap + slot_index // 2
    slot_match = slot_target[:, None] == jnp.arange(devices * half_cap, dtype=jnp.int32)[None, :]
    dispatch = jnp.sum(slot_match.reshape(tok_rows, TOP, -1).astype(jnp.float32), axis=1).astype(
        jnp.bfloat16
    )
    combine_weights = jnp.sum(
        jnp.where(slot_match, route_weights[0].reshape(-1)[:, None], 0.0).reshape(
            tok_rows, TOP, -1
        ),
        axis=1,
    )
    outgoing = lax.dot_general(
        dispatch, normalized, (((0,), (0,)), ((), ())), preferred_element_type=jnp.float32
    ).astype(jnp.bfloat16)
    arrived = lax.all_to_all(outgoing, ("req", "blk"), split_axis=0, concat_axis=0, tiled=True)
    mine = half_expert(arrived, w_gate_up[0], w_down[0])
    other = half_expert(arrived, other_gate_up, other_down)
    both = (mine.astype(jnp.float32) + other.astype(jnp.float32)).astype(jnp.bfloat16)
    returned = lax.all_to_all(both, ("req", "blk"), split_axis=0, concat_axis=0, tiled=True)
    expert_sum = jnp.dot(
        combine_weights,
        returned.astype(jnp.float32),
        precision=lax.Precision.HIGHEST,
        preferred_element_type=jnp.float32,
    )
    return (residual + expert_sum).astype(jnp.bfloat16)[None]


def solution(mesh):
    in_specs = (
        P("req", "blk", None),
        P("req", "blk", None),
        P("req", "blk", None),
        P("req", "blk", None),
        P("req", "blk", None),
        P("req"),
        P("req", "blk", None),
        P(),
        P(),
        P("req", "blk", None),
        P("req", "blk", None),
        P(("req", "blk"), None, None),
        P(("req", "blk"), None, None),
    )
    out_specs = P("req", "blk", None)
    return jax.shard_map(local, mesh=mesh, in_specs=in_specs, out_specs=out_specs, check_vma=False)
```

```python
import math

import jax
import jax.numpy as jnp
from jax import lax
from jax.experimental import pallas as pl
from jax.experimental.pallas import tpu as pltpu
from jax.sharding import PartitionSpec as P

D = 2048
HEADS = 16
KV_HEADS = 4
HEAD_DIM = 128
EXPERTS = 64
TOP = 6


CHUNK = 512


def attn_kernel(s_ref, q_ref, k_ref, v_ref, o_ref):
    group_size = HEADS // KV_HEADS
    tok_rows = q_ref.shape[0]
    rows = tok_rows * group_size
    per_dev = k_ref.shape[1]
    span_len = per_dev - s_ref[2]
    cache_len = s_ref[2]
    length = s_ref[0]
    blk = s_ref[1] + pl.program_id(1)
    qb = q_ref[...]
    qs = jnp.concatenate([qb[:, r * HEAD_DIM:(r + 1) * HEAD_DIM] for r in range(group_size)], axis=0)
    qpos = blk * tok_rows + lax.broadcasted_iota(jnp.int32, (rows, 1), 0) % tok_rows
    col = lax.broadcasted_iota(jnp.int32, (1, CHUNK), 1)
    cache_devs = CHUNK // CACHE_ROWS
    span_devs = CHUNK // SPAN_ROWS
    n_cache = (length + CHUNK - 1) // CHUNK
    n_span = (blk * tok_rows + tok_rows - 1) // CHUNK + 1
    scale = math.sqrt(HEAD_DIM)

    def cache_rows(ref, c):
        return ref[pl.ds(c * cache_devs, cache_devs), pl.ds(0, CACHE_ROWS), :].reshape(CHUNK, HEAD_DIM)

    def span_rows(ref, c):
        return ref[pl.ds(c * span_devs, span_devs), pl.ds(CACHE_ROWS, SPAN_ROWS), :].reshape(CHUNK, HEAD_DIM)

    def scores(k):
        return lax.dot_general(qs, k, (((1,), (1,)), ((), ())), preferred_element_type=jnp.float32) / scale

    def cache_mask(c):
        return (c * CHUNK + col) < length

    def span_mask(c):
        return (c * CHUNK + col) <= qpos

    def peak_step(rows_of, mask_of):
        def body(c, m):
            s = jnp.where(mask_of(c), scores(rows_of(k_ref, c)), -1e30)
            return jnp.maximum(m, jnp.max(s, axis=-1, keepdims=True))
        return body

    m = jnp.full((rows, 1), -1e30, jnp.float32)
    m = lax.fori_loop(0, n_cache, peak_step(cache_rows, cache_mask), m)
    m = lax.fori_loop(0, n_span, peak_step(span_rows, span_mask), m)

    def sum_step(rows_of, mask_of):
        def body(c, carry):
            l, acc = carry
            mask = mask_of(c)
            s = jnp.where(mask, scores(rows_of(k_ref, c)), -1e30)
            p = jnp.where(mask, jnp.exp(s - m), 0.0)
            l = l + jnp.sum(p, axis=-1, keepdims=True)
            acc = acc + jnp.dot(p.astype(jnp.bfloat16), rows_of(v_ref, c), preferred_element_type=jnp.float32)
            return l, acc
        return body

    carry = (jnp.zeros((rows, 1), jnp.float32), jnp.zeros((rows, HEAD_DIM), jnp.float32))
    carry = lax.fori_loop(0, n_cache, sum_step(cache_rows, cache_mask), carry)
    l, acc = lax.fori_loop(0, n_span, sum_step(span_rows, span_mask), carry)
    out = (acc / l).astype(o_ref.dtype)
    for r in range(group_size):
        o_ref[:, r * HEAD_DIM:(r + 1) * HEAD_DIM] = out[r * tok_rows:(r + 1) * tok_rows]


CACHE_ROWS = 128
SPAN_ROWS = 64


def attention(scalars, queries, kv, tok_rows):
    groups = queries.shape[1] // (HEAD_DIM * HEADS // KV_HEADS)
    halves = queries.shape[0] // tok_rows
    devs, per_dev, _ = kv.shape
    group_cols = HEAD_DIM * HEADS // KV_HEADS
    return pl.pallas_call(
        attn_kernel,
        out_shape=jax.ShapeDtypeStruct(queries.shape, jnp.bfloat16),
        grid=(groups, halves),
        in_specs=[
            pl.BlockSpec(memory_space=pltpu.SMEM),
            pl.BlockSpec((tok_rows, group_cols), lambda g, h: (h, g)),
            pl.BlockSpec((devs, per_dev, HEAD_DIM), lambda g, h: (0, 0, g)),
            pl.BlockSpec((devs, per_dev, HEAD_DIM), lambda g, h: (0, 0, groups + g)),
        ],
        out_specs=pl.BlockSpec((tok_rows, group_cols), lambda g, h: (h, g)),
        compiler_params=pltpu.CompilerParams(
            dimension_semantics=("arbitrary", "arbitrary"), vmem_limit_bytes=40 * 1024 * 1024
        ),
    )(scalars, queries, kv, kv)


def half_expert(arrived, gate_up, down_rows):
    half_width = down_rows.shape[0]
    hidden = jnp.dot(arrived, gate_up.T, preferred_element_type=jnp.float32)
    activated = (jax.nn.silu(hidden[:, :half_width]) * hidden[:, half_width:]).astype(jnp.bfloat16)
    return jnp.dot(activated, down_rows, preferred_element_type=jnp.float32).astype(jnp.bfloat16)


def local(
    queries,
    span_keys,
    span_values,
    cache_keys,
    cache_values,
    lengths,
    inputs,
    w_out,
    norm_gain,
    route_ids,
    route_weights,
    w_gate_up,
    w_down,
):
    tok_rows = queries.shape[1]
    blk_count = lax.axis_size("blk")
    blk_index = lax.axis_index("blk")
    length = lengths[0]
    cache_len = cache_keys.shape[1]
    span_len = span_keys.shape[1]

    pairs = [(b, b ^ 1) for b in range(blk_count)]
    other_gate_up = lax.ppermute(w_gate_up[0], "blk", pairs)
    other_down = lax.ppermute(w_down[0], "blk", pairs)

    core = blk_index % 2
    half_cols = KV_HEADS * HEAD_DIM // 2
    key_rows = jnp.concatenate([cache_keys[0], span_keys[0]], 0)
    value_rows = jnp.concatenate([cache_values[0], span_values[0]], 0)

    def kv_cols(which):
        return jnp.concatenate(
            [
                lax.dynamic_slice_in_dim(key_rows, which * half_cols, half_cols, 1),
                lax.dynamic_slice_in_dim(value_rows, which * half_cols, half_cols, 1),
            ],
            1,
        )

    q_cols = queries.shape[2] // 2
    own_q = lax.dynamic_slice_in_dim(queries[0], core * q_cols, q_cols, 1)
    sent_q = lax.dynamic_slice_in_dim(queries[0], (1 - core) * q_cols, q_cols, 1)
    own_kv = kv_cols(core)
    got_kv, got_q = lax.ppermute((kv_cols(1 - core), sent_q), "blk", pairs)
    first = core == 0
    chip_kv = jnp.where(first, jnp.stack([own_kv, got_kv]), jnp.stack([got_kv, own_kv]))
    chip_q = jnp.where(first, jnp.concatenate([own_q, got_q], 0), jnp.concatenate([got_q, own_q], 0))
    same_core = [list(range(0, blk_count, 2)), list(range(1, blk_count, 2))]
    kv = lax.all_gather(chip_kv, "blk", axis=0, tiled=True, axis_index_groups=same_core)
    scalars = jnp.stack(
        [length, (blk_index - core).astype(jnp.int32), jnp.int32(cache_len)]
    )
    chip_out = attention(scalars, chip_q, kv, tok_rows)
    own_out = lax.dynamic_slice_in_dim(chip_out, core * tok_rows, tok_rows, 0)
    sent_out = lax.dynamic_slice_in_dim(chip_out, (1 - core) * tok_rows, tok_rows, 0)
    got_out = lax.ppermute(sent_out, "blk", pairs)
    attended = jnp.where(
        first, jnp.concatenate([own_out, got_out], 1), jnp.concatenate([got_out, own_out], 1)
    )

    residual = inputs[0].astype(jnp.float32) + jnp.dot(
        attended, w_out, preferred_element_type=jnp.float32
    )
    normalized = (
        residual
        * lax.rsqrt(jnp.mean(residual * residual, axis=-1, keepdims=True) + 1e-06)
        * norm_gain
    ).astype(jnp.bfloat16)

    devices = lax.axis_size("req") * blk_count
    capacity = max(2, tok_rows * TOP * 2 // EXPERTS)
    half_cap = (capacity + 1) // 2
    flat_ids = route_ids[0].reshape(-1)
    onehot = (flat_ids[:, None] == jnp.arange(EXPERTS, dtype=jnp.int32)[None, :]).astype(jnp.int32)
    slot_index = jnp.sum((jnp.cumsum(onehot, axis=0) - onehot) * onehot, axis=1)
    slot_target = (2 * flat_ids + slot_index % 2) * half_cap + slot_index // 2
    slot_match = slot_target[:, None] == jnp.arange(devices * half_cap, dtype=jnp.int32)[None, :]
    dispatch = jnp.sum(slot_match.reshape(tok_rows, TOP, -1).astype(jnp.float32), axis=1).astype(
        jnp.bfloat16
    )
    combine_weights = jnp.sum(
        jnp.where(slot_match, route_weights[0].reshape(-1)[:, None], 0.0).reshape(
            tok_rows, TOP, -1
        ),
        axis=1,
    )
    outgoing = lax.dot_general(
        dispatch, normalized, (((0,), (0,)), ((), ())), preferred_element_type=jnp.float32
    ).astype(jnp.bfloat16)
    arrived = lax.all_to_all(outgoing, ("req", "blk"), split_axis=0, concat_axis=0, tiled=True)
    mine = half_expert(arrived, w_gate_up[0], w_down[0])
    other = half_expert(arrived, other_gate_up, other_down)
    both = (mine.astype(jnp.float32) + other.astype(jnp.float32)).astype(jnp.bfloat16)
    returned = lax.all_to_all(both, ("req", "blk"), split_axis=0, concat_axis=0, tiled=True)
    expert_sum = jnp.dot(
        combine_weights,
        returned.astype(jnp.float32),
        precision=lax.Precision.HIGHEST,
        preferred_element_type=jnp.float32,
    )
    return (residual + expert_sum).astype(jnp.bfloat16)[None]


def solution(mesh):
    in_specs = (
        P("req", "blk", None),
        P("req", "blk", None),
        P("req", "blk", None),
        P("req", "blk", None),
        P("req", "blk", None),
        P("req"),
        P("req", "blk", None),
        P(),
        P(),
        P("req", "blk", None),
        P("req", "blk", None),
        P(("req", "blk"), None, None),
        P(("req", "blk"), None, None),
    )
    out_specs = P("req", "blk", None)
    return jax.shard_map(local, mesh=mesh, in_specs=in_specs, out_specs=out_specs, check_vma=False)
```

```python
import math

import jax
import jax.numpy as jnp
from jax import lax
from jax.experimental import pallas as pl
from jax.experimental.pallas import tpu as pltpu
from jax.sharding import PartitionSpec as P

D = 2048
HEADS = 16
KV_HEADS = 4
HEAD_DIM = 128
EXPERTS = 64
TOP = 6


CHUNK = 512


def attn_kernel(s_ref, q_ref, k_ref, v_ref, o_ref):
    group_size = HEADS // KV_HEADS
    tok_rows = q_ref.shape[0]
    rows = tok_rows * group_size
    length = s_ref[0]
    blk = s_ref[1] + pl.program_id(1)
    qb = q_ref[...]
    qs = jnp.concatenate([qb[:, r * HEAD_DIM:(r + 1) * HEAD_DIM] for r in range(group_size)], axis=0)
    qpos = blk * tok_rows + lax.broadcasted_iota(jnp.int32, (rows, 1), 0) % tok_rows
    col = lax.broadcasted_iota(jnp.int32, (1, CHUNK), 1)
    cache_devs = CHUNK // CACHE_ROWS
    span_devs = CHUNK // SPAN_ROWS
    n_cache = (length + CHUNK - 1) // CHUNK
    n_span = (blk * tok_rows + tok_rows - 1) // CHUNK + 1
    scale = math.sqrt(HEAD_DIM)

    def cache_rows(ref, c):
        return ref[pl.ds(c * cache_devs, cache_devs), pl.ds(0, CACHE_ROWS), :].reshape(CHUNK, HEAD_DIM)

    def span_rows(ref, c):
        return ref[pl.ds(c * span_devs, span_devs), pl.ds(CACHE_ROWS, SPAN_ROWS), :].reshape(CHUNK, HEAD_DIM)

    def scores(k):
        return lax.dot_general(qs, k, (((1,), (1,)), ((), ())), preferred_element_type=jnp.float32) / scale

    def cache_mask(c):
        return (c * CHUNK + col) < length

    def span_mask(c):
        return (c * CHUNK + col) <= qpos

    def step(rows_of, mask_of):
        def body(c, carry):
            m, l, acc = carry
            s = scores(rows_of(k_ref, c))
            if mask_of is not None:
                s = jnp.where(mask_of(c), s, -1e30)
            m_new = jnp.maximum(m, jnp.max(s, axis=-1, keepdims=True))
            alpha = jnp.exp(m - m_new)
            p = jnp.exp(s - m_new)
            l = alpha * l + jnp.sum(p, axis=-1, keepdims=True)
            acc = alpha * acc + jnp.dot(
                p.astype(jnp.bfloat16), rows_of(v_ref, c), preferred_element_type=jnp.float32
            )
            return m_new, l, acc
        return body

    carry = (
        jnp.full((rows, 1), -1e30, jnp.float32),
        jnp.zeros((rows, 1), jnp.float32),
        jnp.zeros((rows, HEAD_DIM), jnp.float32),
    )
    cache_full = length // CHUNK
    span_full = (blk * tok_rows + 1) // CHUNK
    carry = lax.fori_loop(0, cache_full, step(cache_rows, None), carry)
    carry = lax.fori_loop(cache_full, n_cache, step(cache_rows, cache_mask), carry)
    carry = lax.fori_loop(0, span_full, step(span_rows, None), carry)
    _, l, acc = lax.fori_loop(span_full, n_span, step(span_rows, span_mask), carry)
    out = (acc / l).astype(o_ref.dtype)
    for r in range(group_size):
        o_ref[:, r * HEAD_DIM:(r + 1) * HEAD_DIM] = out[r * tok_rows:(r + 1) * tok_rows]


CACHE_ROWS = 128
SPAN_ROWS = 64


def attention(scalars, queries, kv, tok_rows):
    groups = queries.shape[1] // (HEAD_DIM * HEADS // KV_HEADS)
    halves = queries.shape[0] // tok_rows
    devs, per_dev, _ = kv.shape
    group_cols = HEAD_DIM * HEADS // KV_HEADS
    return pl.pallas_call(
        attn_kernel,
        out_shape=jax.ShapeDtypeStruct(queries.shape, jnp.bfloat16),
        grid=(groups, halves),
        in_specs=[
            pl.BlockSpec(memory_space=pltpu.SMEM),
            pl.BlockSpec((tok_rows, group_cols), lambda g, h: (h, g)),
            pl.BlockSpec((devs, per_dev, HEAD_DIM), lambda g, h: (0, 0, g)),
            pl.BlockSpec((devs, per_dev, HEAD_DIM), lambda g, h: (0, 0, groups + g)),
        ],
        out_specs=pl.BlockSpec((tok_rows, group_cols), lambda g, h: (h, g)),
        compiler_params=pltpu.CompilerParams(
            dimension_semantics=("arbitrary", "arbitrary"), vmem_limit_bytes=40 * 1024 * 1024
        ),
    )(scalars, queries, kv, kv)


def half_expert(arrived, gate_up, down_rows):
    half_width = down_rows.shape[0]
    hidden = jnp.dot(arrived, gate_up.T, preferred_element_type=jnp.float32)
    activated = (jax.nn.silu(hidden[:, :half_width]) * hidden[:, half_width:]).astype(jnp.bfloat16)
    return jnp.dot(activated, down_rows, preferred_element_type=jnp.float32).astype(jnp.bfloat16)


def local(
    queries,
    span_keys,
    span_values,
    cache_keys,
    cache_values,
    lengths,
    inputs,
    w_out,
    norm_gain,
    route_ids,
    route_weights,
    w_gate_up,
    w_down,
):
    tok_rows = queries.shape[1]
    blk_count = lax.axis_size("blk")
    blk_index = lax.axis_index("blk")
    length = lengths[0]
    cache_len = cache_keys.shape[1]
    span_len = span_keys.shape[1]

    pairs = [(b, b ^ 1) for b in range(blk_count)]
    other_gate_up = lax.ppermute(w_gate_up[0], "blk", pairs)
    other_down = lax.ppermute(w_down[0], "blk", pairs)

    core = blk_index % 2
    half_cols = KV_HEADS * HEAD_DIM // 2
    key_rows = jnp.concatenate([cache_keys[0], span_keys[0]], 0)
    value_rows = jnp.concatenate([cache_values[0], span_values[0]], 0)

    def kv_cols(which):
        return jnp.concatenate(
            [
                lax.dynamic_slice_in_dim(key_rows, which * half_cols, half_cols, 1),
                lax.dynamic_slice_in_dim(value_rows, which * half_cols, half_cols, 1),
            ],
            1,
        )

    q_cols = queries.shape[2] // 2
    own_q = lax.dynamic_slice_in_dim(queries[0], core * q_cols, q_cols, 1)
    sent_q = lax.dynamic_slice_in_dim(queries[0], (1 - core) * q_cols, q_cols, 1)
    own_kv = kv_cols(core)
    got_kv, got_q = lax.ppermute((kv_cols(1 - core), sent_q), "blk", pairs)
    first = core == 0
    chip_kv = jnp.where(first, jnp.stack([own_kv, got_kv]), jnp.stack([got_kv, own_kv]))
    chip_q = jnp.where(first, jnp.concatenate([own_q, got_q], 0), jnp.concatenate([got_q, own_q], 0))
    same_core = [list(range(0, blk_count, 2)), list(range(1, blk_count, 2))]
    kv = lax.all_gather(chip_kv, "blk", axis=0, tiled=True, axis_index_groups=same_core)
    scalars = jnp.stack(
        [length, (blk_index - core).astype(jnp.int32), jnp.int32(cache_len)]
    )
    chip_out = attention(scalars, chip_q, kv, tok_rows)
    own_out = lax.dynamic_slice_in_dim(chip_out, core * tok_rows, tok_rows, 0)
    sent_out = lax.dynamic_slice_in_dim(chip_out, (1 - core) * tok_rows, tok_rows, 0)
    got_out = lax.ppermute(sent_out, "blk", pairs)
    attended = jnp.where(
        first, jnp.concatenate([own_out, got_out], 1), jnp.concatenate([got_out, own_out], 1)
    )

    residual = inputs[0].astype(jnp.float32) + jnp.dot(
        attended, w_out, preferred_element_type=jnp.float32
    )
    normalized = (
        residual
        * lax.rsqrt(jnp.mean(residual * residual, axis=-1, keepdims=True) + 1e-06)
        * norm_gain
    ).astype(jnp.bfloat16)

    devices = lax.axis_size("req") * blk_count
    capacity = max(2, tok_rows * TOP * 2 // EXPERTS)
    half_cap = (capacity + 1) // 2
    flat_ids = route_ids[0].reshape(-1)
    onehot = (flat_ids[:, None] == jnp.arange(EXPERTS, dtype=jnp.int32)[None, :]).astype(jnp.int32)
    slot_index = jnp.sum((jnp.cumsum(onehot, axis=0) - onehot) * onehot, axis=1)
    slot_target = (2 * flat_ids + slot_index % 2) * half_cap + slot_index // 2
    slot_match = slot_target[:, None] == jnp.arange(devices * half_cap, dtype=jnp.int32)[None, :]
    dispatch = jnp.sum(slot_match.reshape(tok_rows, TOP, -1).astype(jnp.float32), axis=1).astype(
        jnp.bfloat16
    )
    combine_weights = jnp.sum(
        jnp.where(slot_match, route_weights[0].reshape(-1)[:, None], 0.0).reshape(
            tok_rows, TOP, -1
        ),
        axis=1,
    )
    outgoing = lax.dot_general(
        dispatch, normalized, (((0,), (0,)), ((), ())), preferred_element_type=jnp.float32
    ).astype(jnp.bfloat16)
    arrived = lax.all_to_all(outgoing, ("req", "blk"), split_axis=0, concat_axis=0, tiled=True)
    mine = half_expert(arrived, w_gate_up[0], w_down[0])
    other = half_expert(arrived, other_gate_up, other_down)
    both = (mine.astype(jnp.float32) + other.astype(jnp.float32)).astype(jnp.bfloat16)
    returned = lax.all_to_all(both, ("req", "blk"), split_axis=0, concat_axis=0, tiled=True)
    expert_sum = jnp.dot(
        combine_weights,
        returned.astype(jnp.float32),
        precision=lax.Precision.HIGHEST,
        preferred_element_type=jnp.float32,
    )
    return (residual + expert_sum).astype(jnp.bfloat16)[None]


def solution(mesh):
    in_specs = (
        P("req", "blk", None),
        P("req", "blk", None),
        P("req", "blk", None),
        P("req", "blk", None),
        P("req", "blk", None),
        P("req"),
        P("req", "blk", None),
        P(),
        P(),
        P("req", "blk", None),
        P("req", "blk", None),
        P(("req", "blk"), None, None),
        P(("req", "blk"), None, None),
    )
    out_specs = P("req", "blk", None)
    return jax.shard_map(local, mesh=mesh, in_specs=in_specs, out_specs=out_specs, check_vma=False)
```

```python
import math

import jax
import jax.numpy as jnp
from jax import lax
from jax.experimental import pallas as pl
from jax.experimental.pallas import tpu as pltpu
from jax.sharding import PartitionSpec as P

D = 2048
HEADS = 16
KV_HEADS = 4
HEAD_DIM = 128
EXPERTS = 64
TOP = 6


CHUNK = 512


def attn_kernel(s_ref, q_ref, k_ref, v_ref, o_ref):
    group_size = HEADS // KV_HEADS
    tok_rows = q_ref.shape[0]
    rows = tok_rows * group_size
    length = s_ref[0]
    blk = s_ref[1] + pl.program_id(1)
    qb = q_ref[...]
    qs = jnp.concatenate([qb[:, r * HEAD_DIM:(r + 1) * HEAD_DIM] for r in range(group_size)], axis=0)
    qpos = blk * tok_rows + lax.broadcasted_iota(jnp.int32, (rows, 1), 0) % tok_rows
    col = lax.broadcasted_iota(jnp.int32, (1, CHUNK), 1)
    cache_devs = CHUNK // CACHE_ROWS
    span_devs = CHUNK // SPAN_ROWS
    n_cache = (length + CHUNK - 1) // CHUNK
    n_span = (blk * tok_rows + tok_rows - 1) // CHUNK + 1
    scale = math.sqrt(HEAD_DIM)

    def cache_rows(ref, c):
        return ref[pl.ds(c * cache_devs, cache_devs), pl.ds(0, CACHE_ROWS), :].reshape(CHUNK, HEAD_DIM)

    def span_rows(ref, c):
        return ref[pl.ds(c * span_devs, span_devs), pl.ds(CACHE_ROWS, SPAN_ROWS), :].reshape(CHUNK, HEAD_DIM)

    def scores(k):
        return lax.dot_general(qs, k, (((1,), (1,)), ((), ())), preferred_element_type=jnp.float32) / scale

    def cache_mask(c):
        return (c * CHUNK + col) < length

    def span_mask(c):
        return (c * CHUNK + col) <= qpos

    def step(rows_of, mask_of):
        def body(c, carry):
            m, l, acc = carry
            s = scores(rows_of(k_ref, c))
            if mask_of is not None:
                s = jnp.where(mask_of(c), s, -1e30)
            m_new = jnp.maximum(m, jnp.max(s, axis=-1, keepdims=True))
            alpha = jnp.exp(m - m_new)
            p = jnp.exp(s - m_new)
            l = alpha * l + jnp.sum(p, axis=-1, keepdims=True)
            acc = alpha * acc + jnp.dot(
                p.astype(jnp.bfloat16), rows_of(v_ref, c), preferred_element_type=jnp.float32
            )
            return m_new, l, acc
        return body

    carry = (
        jnp.full((rows, 1), -1e30, jnp.float32),
        jnp.zeros((rows, 1), jnp.float32),
        jnp.zeros((rows, HEAD_DIM), jnp.float32),
    )
    cache_full = length // CHUNK
    span_full = (blk * tok_rows + 1) // CHUNK
    carry = lax.fori_loop(0, cache_full, step(cache_rows, None), carry)
    carry = lax.fori_loop(cache_full, n_cache, step(cache_rows, cache_mask), carry)
    carry = lax.fori_loop(0, span_full, step(span_rows, None), carry)
    _, l, acc = lax.fori_loop(span_full, n_span, step(span_rows, span_mask), carry)
    out = (acc / l).astype(o_ref.dtype)
    for r in range(group_size):
        o_ref[:, r * HEAD_DIM:(r + 1) * HEAD_DIM] = out[r * tok_rows:(r + 1) * tok_rows]


CACHE_ROWS = 128
SPAN_ROWS = 64


def attention(scalars, queries, kv, tok_rows):
    groups = queries.shape[1] // (HEAD_DIM * HEADS // KV_HEADS)
    halves = queries.shape[0] // tok_rows
    devs, per_dev, _ = kv.shape
    group_cols = HEAD_DIM * HEADS // KV_HEADS
    return pl.pallas_call(
        attn_kernel,
        out_shape=jax.ShapeDtypeStruct(queries.shape, jnp.bfloat16),
        grid=(groups, halves),
        in_specs=[
            pl.BlockSpec(memory_space=pltpu.SMEM),
            pl.BlockSpec((tok_rows, group_cols), lambda g, h: (h, g)),
            pl.BlockSpec((devs, per_dev, HEAD_DIM), lambda g, h: (0, 0, g)),
            pl.BlockSpec((devs, per_dev, HEAD_DIM), lambda g, h: (0, 0, groups + g)),
        ],
        out_specs=pl.BlockSpec((tok_rows, group_cols), lambda g, h: (h, g)),
        compiler_params=pltpu.CompilerParams(
            dimension_semantics=("arbitrary", "arbitrary"), vmem_limit_bytes=40 * 1024 * 1024
        ),
    )(scalars, queries, kv, kv)


def half_expert(arrived, gate_up, down_rows):
    half_width = down_rows.shape[0]
    hidden = jnp.dot(arrived, gate_up.T, preferred_element_type=jnp.float32)
    activated = (jax.nn.silu(hidden[:, :half_width]) * hidden[:, half_width:]).astype(jnp.bfloat16)
    return jnp.dot(activated, down_rows, preferred_element_type=jnp.float32).astype(jnp.bfloat16)


def plane_gather(block, blk_index):
    chips = lax.axis_size("blk") // 2
    side = math.isqrt(chips)
    chip = blk_index // 2
    row, col = chip // side, chip % side
    pieces = [block]
    sources = [chip]
    for dy in range(side):
        for dx in range(side):
            if dy == 0 and dx == 0:
                continue
            perm = []
            for c in range(chips):
                y, x = c // side, c % side
                target = ((y + dy) % side) * side + (x + dx) % side
                for core in range(2):
                    perm.append((c * 2 + core, target * 2 + core))
            pieces.append(lax.ppermute(block, "blk", perm))
            sources.append(((row - dy) % side) * side + (col - dx) % side)
    stacked = jnp.stack(pieces)
    order = jnp.argsort(jnp.stack(sources))
    return jnp.take(stacked, order, axis=0)


def local(
    queries,
    span_keys,
    span_values,
    cache_keys,
    cache_values,
    lengths,
    inputs,
    w_out,
    norm_gain,
    route_ids,
    route_weights,
    w_gate_up,
    w_down,
):
    tok_rows = queries.shape[1]
    blk_count = lax.axis_size("blk")
    blk_index = lax.axis_index("blk")
    length = lengths[0]
    cache_len = cache_keys.shape[1]
    span_len = span_keys.shape[1]

    pairs = [(b, b ^ 1) for b in range(blk_count)]
    other_gate_up = lax.ppermute(w_gate_up[0], "blk", pairs)
    other_down = lax.ppermute(w_down[0], "blk", pairs)

    core = blk_index % 2
    half_cols = KV_HEADS * HEAD_DIM // 2
    key_rows = jnp.concatenate([cache_keys[0], span_keys[0]], 0)
    value_rows = jnp.concatenate([cache_values[0], span_values[0]], 0)

    def kv_cols(which):
        return jnp.concatenate(
            [
                lax.dynamic_slice_in_dim(key_rows, which * half_cols, half_cols, 1),
                lax.dynamic_slice_in_dim(value_rows, which * half_cols, half_cols, 1),
            ],
            1,
        )

    q_cols = queries.shape[2] // 2
    own_q = lax.dynamic_slice_in_dim(queries[0], core * q_cols, q_cols, 1)
    sent_q = lax.dynamic_slice_in_dim(queries[0], (1 - core) * q_cols, q_cols, 1)
    own_kv = kv_cols(core)
    got_kv, got_q = lax.ppermute((kv_cols(1 - core), sent_q), "blk", pairs)
    first = core == 0
    chip_kv = jnp.where(first, jnp.stack([own_kv, got_kv]), jnp.stack([got_kv, own_kv]))
    chip_q = jnp.where(first, jnp.concatenate([own_q, got_q], 0), jnp.concatenate([got_q, own_q], 0))
    kv = plane_gather(chip_kv, blk_index).reshape(-1, *chip_kv.shape[1:])
    scalars = jnp.stack(
        [length, (blk_index - core).astype(jnp.int32), jnp.int32(cache_len)]
    )
    chip_out = attention(scalars, chip_q, kv, tok_rows)
    own_out = lax.dynamic_slice_in_dim(chip_out, core * tok_rows, tok_rows, 0)
    sent_out = lax.dynamic_slice_in_dim(chip_out, (1 - core) * tok_rows, tok_rows, 0)
    got_out = lax.ppermute(sent_out, "blk", pairs)
    attended = jnp.where(
        first, jnp.concatenate([own_out, got_out], 1), jnp.concatenate([got_out, own_out], 1)
    )

    residual = inputs[0].astype(jnp.float32) + jnp.dot(
        attended, w_out, preferred_element_type=jnp.float32
    )
    normalized = (
        residual
        * lax.rsqrt(jnp.mean(residual * residual, axis=-1, keepdims=True) + 1e-06)
        * norm_gain
    ).astype(jnp.bfloat16)

    devices = lax.axis_size("req") * blk_count
    capacity = max(2, tok_rows * TOP * 2 // EXPERTS)
    half_cap = (capacity + 1) // 2
    flat_ids = route_ids[0].reshape(-1)
    onehot = (flat_ids[:, None] == jnp.arange(EXPERTS, dtype=jnp.int32)[None, :]).astype(jnp.int32)
    slot_index = jnp.sum((jnp.cumsum(onehot, axis=0) - onehot) * onehot, axis=1)
    slot_target = (2 * flat_ids + slot_index % 2) * half_cap + slot_index // 2
    slot_match = slot_target[:, None] == jnp.arange(devices * half_cap, dtype=jnp.int32)[None, :]
    dispatch = jnp.sum(slot_match.reshape(tok_rows, TOP, -1).astype(jnp.float32), axis=1).astype(
        jnp.bfloat16
    )
    combine_weights = jnp.sum(
        jnp.where(slot_match, route_weights[0].reshape(-1)[:, None], 0.0).reshape(
            tok_rows, TOP, -1
        ),
        axis=1,
    )
    outgoing = lax.dot_general(
        dispatch, normalized, (((0,), (0,)), ((), ())), preferred_element_type=jnp.float32
    ).astype(jnp.bfloat16)
    arrived = lax.all_to_all(outgoing, ("req", "blk"), split_axis=0, concat_axis=0, tiled=True)
    mine = half_expert(arrived, w_gate_up[0], w_down[0])
    other = half_expert(arrived, other_gate_up, other_down)
    both = (mine.astype(jnp.float32) + other.astype(jnp.float32)).astype(jnp.bfloat16)
    returned = lax.all_to_all(both, ("req", "blk"), split_axis=0, concat_axis=0, tiled=True)
    expert_sum = jnp.dot(
        combine_weights,
        returned.astype(jnp.float32),
        precision=lax.Precision.HIGHEST,
        preferred_element_type=jnp.float32,
    )
    return (residual + expert_sum).astype(jnp.bfloat16)[None]


def solution(mesh):
    in_specs = (
        P("req", "blk", None),
        P("req", "blk", None),
        P("req", "blk", None),
        P("req", "blk", None),
        P("req", "blk", None),
        P("req"),
        P("req", "blk", None),
        P(),
        P(),
        P("req", "blk", None),
        P("req", "blk", None),
        P(("req", "blk"), None, None),
        P(("req", "blk"), None, None),
    )
    out_specs = P("req", "blk", None)
    return jax.shard_map(local, mesh=mesh, in_specs=in_specs, out_specs=out_specs, check_vma=False)
```

```python
import math

import jax
import jax.numpy as jnp
from jax import lax
from jax.experimental import pallas as pl
from jax.experimental.pallas import tpu as pltpu
from jax.sharding import PartitionSpec as P

D = 2048
HEADS = 16
KV_HEADS = 4
HEAD_DIM = 128
EXPERTS = 64
TOP = 6


CHUNK = 512


def attn_kernel(s_ref, q_ref, k_ref, v_ref, o_ref):
    group_size = HEADS // KV_HEADS
    tok_rows = q_ref.shape[0]
    rows = tok_rows * group_size
    length = s_ref[0]
    blk = s_ref[1] + pl.program_id(1)
    qb = q_ref[...]
    qs = jnp.concatenate([qb[:, r * HEAD_DIM:(r + 1) * HEAD_DIM] for r in range(group_size)], axis=0)
    qpos = blk * tok_rows + lax.broadcasted_iota(jnp.int32, (rows, 1), 0) % tok_rows
    col = lax.broadcasted_iota(jnp.int32, (1, CHUNK), 1)
    cache_devs = CHUNK // CACHE_ROWS
    span_devs = CHUNK // SPAN_ROWS
    n_cache = (length + CHUNK - 1) // CHUNK
    n_span = (blk * tok_rows + tok_rows - 1) // CHUNK + 1
    scale = math.sqrt(HEAD_DIM)

    def cache_rows(ref, c):
        return ref[pl.ds(c * cache_devs, cache_devs), pl.ds(0, CACHE_ROWS), :].reshape(CHUNK, HEAD_DIM)

    def span_rows(ref, c):
        return ref[pl.ds(c * span_devs, span_devs), pl.ds(CACHE_ROWS, SPAN_ROWS), :].reshape(CHUNK, HEAD_DIM)

    def scores(k):
        return lax.dot_general(qs, k, (((1,), (1,)), ((), ())), preferred_element_type=jnp.float32) / scale

    def cache_mask(c):
        return (c * CHUNK + col) < length

    def span_mask(c):
        return (c * CHUNK + col) <= qpos

    def step(rows_of, mask_of):
        def body(c, carry):
            m, l, acc = carry
            s = scores(rows_of(k_ref, c))
            if mask_of is not None:
                s = jnp.where(mask_of(c), s, -1e30)
            m_new = jnp.maximum(m, jnp.max(s, axis=-1, keepdims=True))
            alpha = jnp.exp(m - m_new)
            p = jnp.exp(s - m_new)
            l = alpha * l + jnp.sum(p, axis=-1, keepdims=True)
            acc = alpha * acc + jnp.dot(
                p.astype(jnp.bfloat16), rows_of(v_ref, c), preferred_element_type=jnp.float32
            )
            return m_new, l, acc
        return body

    carry = (
        jnp.full((rows, 1), -1e30, jnp.float32),
        jnp.zeros((rows, 1), jnp.float32),
        jnp.zeros((rows, HEAD_DIM), jnp.float32),
    )
    cache_full = length // CHUNK
    span_full = (blk * tok_rows + 1) // CHUNK
    carry = lax.fori_loop(0, cache_full, step(cache_rows, None), carry)
    carry = lax.fori_loop(cache_full, n_cache, step(cache_rows, cache_mask), carry)
    carry = lax.fori_loop(0, span_full, step(span_rows, None), carry)
    _, l, acc = lax.fori_loop(span_full, n_span, step(span_rows, span_mask), carry)
    out = (acc / l).astype(o_ref.dtype)
    for r in range(group_size):
        o_ref[:, r * HEAD_DIM:(r + 1) * HEAD_DIM] = out[r * tok_rows:(r + 1) * tok_rows]


CACHE_ROWS = 128
SPAN_ROWS = 64


def attention(scalars, queries, kv, tok_rows):
    groups = queries.shape[1] // (HEAD_DIM * HEADS // KV_HEADS)
    halves = queries.shape[0] // tok_rows
    devs, per_dev, _ = kv.shape
    group_cols = HEAD_DIM * HEADS // KV_HEADS
    return pl.pallas_call(
        attn_kernel,
        out_shape=jax.ShapeDtypeStruct(queries.shape, jnp.bfloat16),
        grid=(groups, halves),
        in_specs=[
            pl.BlockSpec(memory_space=pltpu.SMEM),
            pl.BlockSpec((tok_rows, group_cols), lambda g, h: (h, g)),
            pl.BlockSpec((devs, per_dev, HEAD_DIM), lambda g, h: (0, 0, g)),
            pl.BlockSpec((devs, per_dev, HEAD_DIM), lambda g, h: (0, 0, groups + g)),
        ],
        out_specs=pl.BlockSpec((tok_rows, group_cols), lambda g, h: (h, g)),
        compiler_params=pltpu.CompilerParams(
            dimension_semantics=("arbitrary", "arbitrary"), vmem_limit_bytes=40 * 1024 * 1024
        ),
    )(scalars, queries, kv, kv)


def half_expert(arrived, gate_up, down_rows):
    half_width = down_rows.shape[0]
    hidden = jnp.dot(arrived, gate_up.T, preferred_element_type=jnp.float32)
    activated = (jax.nn.silu(hidden[:, :half_width]) * hidden[:, half_width:]).astype(jnp.bfloat16)
    return jnp.dot(activated, down_rows, preferred_element_type=jnp.float32).astype(jnp.bfloat16)


def local(
    queries,
    span_keys,
    span_values,
    cache_keys,
    cache_values,
    lengths,
    inputs,
    w_out,
    norm_gain,
    route_ids,
    route_weights,
    w_gate_up,
    w_down,
):
    tok_rows = queries.shape[1]
    blk_count = lax.axis_size("blk")
    blk_index = lax.axis_index("blk")
    length = lengths[0]
    cache_len = cache_keys.shape[1]
    span_len = span_keys.shape[1]

    pairs = [(b, b ^ 1) for b in range(blk_count)]
    other_gate_up = lax.ppermute(w_gate_up[0], "blk", pairs)
    other_down = lax.ppermute(w_down[0], "blk", pairs)

    core = blk_index % 2
    half_cols = KV_HEADS * HEAD_DIM // 2
    key_rows = jnp.concatenate([cache_keys[0], span_keys[0]], 0)
    value_rows = jnp.concatenate([cache_values[0], span_values[0]], 0)

    def kv_cols(which):
        return jnp.concatenate(
            [
                lax.dynamic_slice_in_dim(key_rows, which * half_cols, half_cols, 1),
                lax.dynamic_slice_in_dim(value_rows, which * half_cols, half_cols, 1),
            ],
            1,
        )

    q_cols = queries.shape[2] // 2
    own_q = lax.dynamic_slice_in_dim(queries[0], core * q_cols, q_cols, 1)
    sent_q = lax.dynamic_slice_in_dim(queries[0], (1 - core) * q_cols, q_cols, 1)
    own_kv = kv_cols(core)
    got_kv, got_q = lax.ppermute((kv_cols(1 - core), sent_q), "blk", pairs)
    first = core == 0
    chip_kv = jnp.where(first, jnp.stack([own_kv, got_kv]), jnp.stack([got_kv, own_kv]))
    chip_q = jnp.where(first, jnp.concatenate([own_q, got_q], 0), jnp.concatenate([got_q, own_q], 0))
    same_core = [list(range(0, blk_count, 2)), list(range(1, blk_count, 2))]
    kv = lax.all_gather(chip_kv, "blk", axis=0, tiled=True, axis_index_groups=same_core)
    scalars = jnp.stack(
        [length, (blk_index - core).astype(jnp.int32), jnp.int32(cache_len)]
    )
    chip_out = attention(scalars, chip_q, kv, tok_rows)
    own_out = lax.dynamic_slice_in_dim(chip_out, core * tok_rows, tok_rows, 0)
    sent_out = lax.dynamic_slice_in_dim(chip_out, (1 - core) * tok_rows, tok_rows, 0)
    got_out = lax.ppermute(sent_out, "blk", pairs)
    attended = jnp.where(
        first, jnp.concatenate([own_out, got_out], 1), jnp.concatenate([got_out, own_out], 1)
    )
    attended, other_gate_up, other_down = lax.optimization_barrier(
        (attended, other_gate_up, other_down)
    )

    residual = inputs[0].astype(jnp.float32) + jnp.dot(
        attended, w_out, preferred_element_type=jnp.float32
    )
    normalized = (
        residual
        * lax.rsqrt(jnp.mean(residual * residual, axis=-1, keepdims=True) + 1e-06)
        * norm_gain
    ).astype(jnp.bfloat16)

    devices = lax.axis_size("req") * blk_count
    capacity = max(2, tok_rows * TOP * 2 // EXPERTS)
    half_cap = -(-((capacity + 1) // 2) // 8) * 8
    flat_ids = route_ids[0].reshape(-1)
    onehot = (flat_ids[:, None] == jnp.arange(EXPERTS, dtype=jnp.int32)[None, :]).astype(jnp.int32)
    slot_index = jnp.sum((jnp.cumsum(onehot, axis=0) - onehot) * onehot, axis=1)
    slot_target = (2 * flat_ids + slot_index % 2) * half_cap + slot_index // 2
    slot_match = slot_target[:, None] == jnp.arange(devices * half_cap, dtype=jnp.int32)[None, :]
    dispatch = jnp.sum(slot_match.reshape(tok_rows, TOP, -1).astype(jnp.float32), axis=1).astype(
        jnp.bfloat16
    )
    combine_weights = jnp.sum(
        jnp.where(slot_match, route_weights[0].reshape(-1)[:, None], 0.0).reshape(
            tok_rows, TOP, -1
        ),
        axis=1,
    )
    outgoing = lax.dot_general(
        dispatch, normalized, (((0,), (0,)), ((), ())), preferred_element_type=jnp.float32
    ).astype(jnp.bfloat16)
    arrived = lax.all_to_all(outgoing, ("req", "blk"), split_axis=0, concat_axis=0, tiled=True)
    mine = half_expert(arrived, w_gate_up[0], w_down[0])
    other = half_expert(arrived, other_gate_up, other_down)
    both = (mine.astype(jnp.float32) + other.astype(jnp.float32)).astype(jnp.bfloat16)
    returned = lax.all_to_all(both, ("req", "blk"), split_axis=0, concat_axis=0, tiled=True)
    expert_sum = jnp.dot(
        combine_weights,
        returned.astype(jnp.float32),
        precision=lax.Precision.HIGHEST,
        preferred_element_type=jnp.float32,
    )
    return (residual + expert_sum).astype(jnp.bfloat16)[None]


def solution(mesh):
    in_specs = (
        P("req", "blk", None),
        P("req", "blk", None),
        P("req", "blk", None),
        P("req", "blk", None),
        P("req", "blk", None),
        P("req"),
        P("req", "blk", None),
        P(),
        P(),
        P("req", "blk", None),
        P("req", "blk", None),
        P(("req", "blk"), None, None),
        P(("req", "blk"), None, None),
    )
    out_specs = P("req", "blk", None)
    return jax.shard_map(local, mesh=mesh, in_specs=in_specs, out_specs=out_specs, check_vma=False)
```

```python
import math

import jax
import jax.numpy as jnp
from jax import lax
from jax.experimental import pallas as pl
from jax.experimental.pallas import tpu as pltpu
from jax.sharding import PartitionSpec as P

D = 2048
HEADS = 16
KV_HEADS = 4
HEAD_DIM = 128
EXPERTS = 64
TOP = 6


CHUNK = 512


def attn_kernel(s_ref, q_ref, k_ref, v_ref, o_ref):
    group_size = HEADS // KV_HEADS
    tok_rows = q_ref.shape[0]
    rows = tok_rows * group_size
    length = s_ref[0]
    blk = s_ref[1] + pl.program_id(1)
    qb = q_ref[...]
    qs = jnp.concatenate([qb[:, r * HEAD_DIM:(r + 1) * HEAD_DIM] for r in range(group_size)], axis=0)
    qpos = blk * tok_rows + lax.broadcasted_iota(jnp.int32, (rows, 1), 0) % tok_rows
    col = lax.broadcasted_iota(jnp.int32, (1, CHUNK), 1)
    cache_devs = CHUNK // CACHE_ROWS
    span_devs = CHUNK // SPAN_ROWS
    n_cache = (length + CHUNK - 1) // CHUNK
    n_span = (blk * tok_rows + tok_rows - 1) // CHUNK + 1
    factor = math.log2(math.e) / math.sqrt(HEAD_DIM)
    ones = jnp.ones((CHUNK, HEAD_DIM), jnp.bfloat16)

    def cache_rows(ref, c):
        return ref[pl.ds(c * cache_devs, cache_devs), pl.ds(0, CACHE_ROWS), :].reshape(CHUNK, HEAD_DIM)

    def span_rows(ref, c):
        return ref[pl.ds(c * span_devs, span_devs), pl.ds(CACHE_ROWS, SPAN_ROWS), :].reshape(CHUNK, HEAD_DIM)

    def scores(k):
        return lax.dot_general(qs, k, (((1,), (1,)), ((), ())), preferred_element_type=jnp.float32)

    def cache_mask(c):
        return (c * CHUNK + col) < length

    def span_mask(c):
        return (c * CHUNK + col) <= qpos

    def step(rows_of, mask_of):
        def body(c, carry):
            m, l, acc = carry
            s = scores(rows_of(k_ref, c))
            if mask_of is not None:
                s = jnp.where(mask_of(c), s, -1e30)
            m_new = jnp.maximum(m, jnp.max(s, axis=-1, keepdims=True))
            alpha = jnp.exp2((m - m_new) * factor)
            p = jnp.exp2((s - m_new) * factor).astype(jnp.bfloat16)
            l = alpha * l + jnp.dot(p, ones, preferred_element_type=jnp.float32)[:, :1]
            acc = alpha * acc + jnp.dot(p, rows_of(v_ref, c), preferred_element_type=jnp.float32)
            return m_new, l, acc
        return body

    carry = (
        jnp.full((rows, 1), -1e30, jnp.float32),
        jnp.zeros((rows, 1), jnp.float32),
        jnp.zeros((rows, HEAD_DIM), jnp.float32),
    )
    cache_full = length // CHUNK
    span_full = (blk * tok_rows + 1) // CHUNK
    carry = lax.fori_loop(0, cache_full, step(cache_rows, None), carry)
    carry = lax.fori_loop(cache_full, n_cache, step(cache_rows, cache_mask), carry)
    carry = lax.fori_loop(0, span_full, step(span_rows, None), carry)
    _, l, acc = lax.fori_loop(span_full, n_span, step(span_rows, span_mask), carry)
    out = (acc / l).astype(o_ref.dtype)
    for r in range(group_size):
        o_ref[:, r * HEAD_DIM:(r + 1) * HEAD_DIM] = out[r * tok_rows:(r + 1) * tok_rows]


CACHE_ROWS = 128
SPAN_ROWS = 64


def attention(scalars, queries, kv, tok_rows):
    groups = queries.shape[1] // (HEAD_DIM * HEADS // KV_HEADS)
    halves = queries.shape[0] // tok_rows
    devs, per_dev, _ = kv.shape
    group_cols = HEAD_DIM * HEADS // KV_HEADS
    return pl.pallas_call(
        attn_kernel,
        out_shape=jax.ShapeDtypeStruct(queries.shape, jnp.bfloat16),
        grid=(groups, halves),
        in_specs=[
            pl.BlockSpec(memory_space=pltpu.SMEM),
            pl.BlockSpec((tok_rows, group_cols), lambda g, h: (h, g)),
            pl.BlockSpec((devs, per_dev, HEAD_DIM), lambda g, h: (0, 0, g)),
            pl.BlockSpec((devs, per_dev, HEAD_DIM), lambda g, h: (0, 0, groups + g)),
        ],
        out_specs=pl.BlockSpec((tok_rows, group_cols), lambda g, h: (h, g)),
        compiler_params=pltpu.CompilerParams(
            dimension_semantics=("arbitrary", "arbitrary"), vmem_limit_bytes=40 * 1024 * 1024
        ),
    )(scalars, queries, kv, kv)


def half_expert(arrived, gate_up, down_rows):
    half_width = down_rows.shape[0]
    hidden = jnp.dot(arrived, gate_up.T, preferred_element_type=jnp.float32)
    activated = (jax.nn.silu(hidden[:, :half_width]) * hidden[:, half_width:]).astype(jnp.bfloat16)
    return jnp.dot(activated, down_rows, preferred_element_type=jnp.float32).astype(jnp.bfloat16)


def local(
    queries,
    span_keys,
    span_values,
    cache_keys,
    cache_values,
    lengths,
    inputs,
    w_out,
    norm_gain,
    route_ids,
    route_weights,
    w_gate_up,
    w_down,
):
    tok_rows = queries.shape[1]
    blk_count = lax.axis_size("blk")
    blk_index = lax.axis_index("blk")
    length = lengths[0]
    cache_len = cache_keys.shape[1]
    span_len = span_keys.shape[1]

    pairs = [(b, b ^ 1) for b in range(blk_count)]
    other_gate_up = lax.ppermute(w_gate_up[0], "blk", pairs)
    other_down = lax.ppermute(w_down[0], "blk", pairs)

    core = blk_index % 2
    half_cols = KV_HEADS * HEAD_DIM // 2
    key_rows = jnp.concatenate([cache_keys[0], span_keys[0]], 0)
    value_rows = jnp.concatenate([cache_values[0], span_values[0]], 0)

    def kv_cols(which):
        return jnp.concatenate(
            [
                lax.dynamic_slice_in_dim(key_rows, which * half_cols, half_cols, 1),
                lax.dynamic_slice_in_dim(value_rows, which * half_cols, half_cols, 1),
            ],
            1,
        )

    q_cols = queries.shape[2] // 2
    own_q = lax.dynamic_slice_in_dim(queries[0], core * q_cols, q_cols, 1)
    sent_q = lax.dynamic_slice_in_dim(queries[0], (1 - core) * q_cols, q_cols, 1)
    own_kv = kv_cols(core)
    got_kv, got_q = lax.ppermute((kv_cols(1 - core), sent_q), "blk", pairs)
    first = core == 0
    chip_kv = jnp.where(first, jnp.stack([own_kv, got_kv]), jnp.stack([got_kv, own_kv]))
    chip_q = jnp.where(first, jnp.concatenate([own_q, got_q], 0), jnp.concatenate([got_q, own_q], 0))
    same_core = [list(range(0, blk_count, 2)), list(range(1, blk_count, 2))]
    kv = lax.all_gather(chip_kv, "blk", axis=0, tiled=True, axis_index_groups=same_core)
    scalars = jnp.stack(
        [length, (blk_index - core).astype(jnp.int32), jnp.int32(cache_len)]
    )
    chip_out = attention(scalars, chip_q, kv, tok_rows)
    own_out = lax.dynamic_slice_in_dim(chip_out, core * tok_rows, tok_rows, 0)
    sent_out = lax.dynamic_slice_in_dim(chip_out, (1 - core) * tok_rows, tok_rows, 0)
    got_out = lax.ppermute(sent_out, "blk", pairs)
    attended = jnp.where(
        first, jnp.concatenate([own_out, got_out], 1), jnp.concatenate([got_out, own_out], 1)
    )
    attended, other_gate_up, other_down = lax.optimization_barrier(
        (attended, other_gate_up, other_down)
    )

    residual = inputs[0].astype(jnp.float32) + jnp.dot(
        attended, w_out, preferred_element_type=jnp.float32
    )
    normalized = (
        residual
        * lax.rsqrt(jnp.mean(residual * residual, axis=-1, keepdims=True) + 1e-06)
        * norm_gain
    ).astype(jnp.bfloat16)

    devices = lax.axis_size("req") * blk_count
    capacity = max(2, tok_rows * TOP * 2 // EXPERTS)
    half_cap = -(-((capacity + 1) // 2) // 8) * 8
    flat_ids = route_ids[0].reshape(-1)
    onehot = (flat_ids[:, None] == jnp.arange(EXPERTS, dtype=jnp.int32)[None, :]).astype(jnp.int32)
    slot_index = jnp.sum((jnp.cumsum(onehot, axis=0) - onehot) * onehot, axis=1)
    slot_target = (2 * flat_ids + slot_index % 2) * half_cap + slot_index // 2
    slot_match = slot_target[:, None] == jnp.arange(devices * half_cap, dtype=jnp.int32)[None, :]
    dispatch = jnp.sum(slot_match.reshape(tok_rows, TOP, -1).astype(jnp.float32), axis=1).astype(
        jnp.bfloat16
    )
    combine_weights = jnp.sum(
        jnp.where(slot_match, route_weights[0].reshape(-1)[:, None], 0.0).reshape(
            tok_rows, TOP, -1
        ),
        axis=1,
    )
    outgoing = lax.dot_general(
        dispatch, normalized, (((0,), (0,)), ((), ())), preferred_element_type=jnp.float32
    ).astype(jnp.bfloat16)
    arrived = lax.all_to_all(outgoing, ("req", "blk"), split_axis=0, concat_axis=0, tiled=True)
    mine = half_expert(arrived, w_gate_up[0], w_down[0])
    other = half_expert(arrived, other_gate_up, other_down)
    both = (mine.astype(jnp.float32) + other.astype(jnp.float32)).astype(jnp.bfloat16)
    returned = lax.all_to_all(both, ("req", "blk"), split_axis=0, concat_axis=0, tiled=True)
    expert_sum = jnp.dot(
        combine_weights,
        returned.astype(jnp.float32),
        precision=lax.Precision.HIGHEST,
        preferred_element_type=jnp.float32,
    )
    return (residual + expert_sum).astype(jnp.bfloat16)[None]


def solution(mesh):
    in_specs = (
        P("req", "blk", None),
        P("req", "blk", None),
        P("req", "blk", None),
        P("req", "blk", None),
        P("req", "blk", None),
        P("req"),
        P("req", "blk", None),
        P(),
        P(),
        P("req", "blk", None),
        P("req", "blk", None),
        P(("req", "blk"), None, None),
        P(("req", "blk"), None, None),
    )
    out_specs = P("req", "blk", None)
    return jax.shard_map(local, mesh=mesh, in_specs=in_specs, out_specs=out_specs, check_vma=False)
```

```python
import math

import jax
import jax.numpy as jnp
from jax import lax
from jax.experimental import pallas as pl
from jax.experimental.pallas import tpu as pltpu
from jax.sharding import PartitionSpec as P

D = 2048
HEADS = 16
KV_HEADS = 4
HEAD_DIM = 128
EXPERTS = 64
TOP = 6


CHUNK = 256


def attn_kernel(s_ref, q_ref, k_ref, v_ref, o_ref):
    group_size = HEADS // KV_HEADS
    tok_rows = q_ref.shape[0]
    rows = tok_rows * group_size
    length = s_ref[0]
    blk = s_ref[1] + pl.program_id(1)
    qb = q_ref[...]
    qs = jnp.concatenate([qb[:, r * HEAD_DIM:(r + 1) * HEAD_DIM] for r in range(group_size)], axis=0)
    qpos = blk * tok_rows + lax.broadcasted_iota(jnp.int32, (rows, 1), 0) % tok_rows
    col = lax.broadcasted_iota(jnp.int32, (1, CHUNK), 1)
    cache_devs = CHUNK // CACHE_ROWS
    span_devs = CHUNK // SPAN_ROWS
    n_cache = (length + CHUNK - 1) // CHUNK
    n_span = (blk * tok_rows + tok_rows - 1) // CHUNK + 1
    factor = math.log2(math.e) / math.sqrt(HEAD_DIM)

    def cache_rows(ref, c):
        return ref[pl.ds(c * cache_devs, cache_devs), pl.ds(0, CACHE_ROWS), :].reshape(CHUNK, HEAD_DIM)

    def span_rows(ref, c):
        return ref[pl.ds(c * span_devs, span_devs), pl.ds(CACHE_ROWS, SPAN_ROWS), :].reshape(CHUNK, HEAD_DIM)

    def scores(k):
        return lax.dot_general(qs, k, (((1,), (1,)), ((), ())), preferred_element_type=jnp.float32)

    def cache_mask(c):
        return (c * CHUNK + col) < length

    def span_mask(c):
        return (c * CHUNK + col) <= qpos

    def step(rows_of, mask_of):
        def body(c, carry):
            m, l, acc = carry
            s = scores(rows_of(k_ref, c))
            if mask_of is not None:
                s = jnp.where(mask_of(c), s, -1e30)
            m_new = jnp.maximum(m, jnp.max(s, axis=-1, keepdims=True))
            alpha = jnp.exp2((m - m_new) * factor)
            p = jnp.exp2((s - m_new) * factor)
            l = alpha * l + jnp.sum(p, axis=-1, keepdims=True)
            acc = alpha * acc + jnp.dot(
                p.astype(jnp.bfloat16), rows_of(v_ref, c), preferred_element_type=jnp.float32
            )
            return m_new, l, acc
        return body

    carry = (
        jnp.full((rows, 1), -1e30, jnp.float32),
        jnp.zeros((rows, 1), jnp.float32),
        jnp.zeros((rows, HEAD_DIM), jnp.float32),
    )
    cache_full = length // CHUNK
    span_full = (blk * tok_rows + 1) // CHUNK
    carry = lax.fori_loop(0, cache_full, step(cache_rows, None), carry)
    carry = lax.fori_loop(cache_full, n_cache, step(cache_rows, cache_mask), carry)
    carry = lax.fori_loop(0, span_full, step(span_rows, None), carry)
    _, l, acc = lax.fori_loop(span_full, n_span, step(span_rows, span_mask), carry)
    out = (acc / l).astype(o_ref.dtype)
    for r in range(group_size):
        o_ref[:, r * HEAD_DIM:(r + 1) * HEAD_DIM] = out[r * tok_rows:(r + 1) * tok_rows]


CACHE_ROWS = 128
SPAN_ROWS = 64


def attention(scalars, queries, kv, tok_rows):
    groups = queries.shape[1] // (HEAD_DIM * HEADS // KV_HEADS)
    halves = queries.shape[0] // tok_rows
    devs, per_dev, _ = kv.shape
    group_cols = HEAD_DIM * HEADS // KV_HEADS
    return pl.pallas_call(
        attn_kernel,
        out_shape=jax.ShapeDtypeStruct(queries.shape, jnp.bfloat16),
        grid=(groups, halves),
        in_specs=[
            pl.BlockSpec(memory_space=pltpu.SMEM),
            pl.BlockSpec((tok_rows, group_cols), lambda g, h: (h, g)),
            pl.BlockSpec((devs, per_dev, HEAD_DIM), lambda g, h: (0, 0, g)),
            pl.BlockSpec((devs, per_dev, HEAD_DIM), lambda g, h: (0, 0, groups + g)),
        ],
        out_specs=pl.BlockSpec((tok_rows, group_cols), lambda g, h: (h, g)),
        compiler_params=pltpu.CompilerParams(
            dimension_semantics=("arbitrary", "arbitrary"), vmem_limit_bytes=40 * 1024 * 1024
        ),
    )(scalars, queries, kv, kv)


def half_expert(arrived, gate_up, down_rows):
    half_width = down_rows.shape[0]
    hidden = jnp.dot(arrived, gate_up.T, preferred_element_type=jnp.float32)
    activated = (jax.nn.silu(hidden[:, :half_width]) * hidden[:, half_width:]).astype(jnp.bfloat16)
    return jnp.dot(activated, down_rows, preferred_element_type=jnp.float32).astype(jnp.bfloat16)


def local(
    queries,
    span_keys,
    span_values,
    cache_keys,
    cache_values,
    lengths,
    inputs,
    w_out,
    norm_gain,
    route_ids,
    route_weights,
    w_gate_up,
    w_down,
):
    tok_rows = queries.shape[1]
    blk_count = lax.axis_size("blk")
    blk_index = lax.axis_index("blk")
    length = lengths[0]
    cache_len = cache_keys.shape[1]
    span_len = span_keys.shape[1]

    pairs = [(b, b ^ 1) for b in range(blk_count)]
    other_gate_up = lax.ppermute(w_gate_up[0], "blk", pairs)
    other_down = lax.ppermute(w_down[0], "blk", pairs)

    core = blk_index % 2
    half_cols = KV_HEADS * HEAD_DIM // 2
    key_rows = jnp.concatenate([cache_keys[0], span_keys[0]], 0)
    value_rows = jnp.concatenate([cache_values[0], span_values[0]], 0)

    def kv_cols(which):
        return jnp.concatenate(
            [
                lax.dynamic_slice_in_dim(key_rows, which * half_cols, half_cols, 1),
                lax.dynamic_slice_in_dim(value_rows, which * half_cols, half_cols, 1),
            ],
            1,
        )

    q_cols = queries.shape[2] // 2
    own_q = lax.dynamic_slice_in_dim(queries[0], core * q_cols, q_cols, 1)
    sent_q = lax.dynamic_slice_in_dim(queries[0], (1 - core) * q_cols, q_cols, 1)
    own_kv = kv_cols(core)
    got_kv, got_q = lax.ppermute((kv_cols(1 - core), sent_q), "blk", pairs)
    first = core == 0
    chip_kv = jnp.where(first, jnp.stack([own_kv, got_kv]), jnp.stack([got_kv, own_kv]))
    chip_q = jnp.where(first, jnp.concatenate([own_q, got_q], 0), jnp.concatenate([got_q, own_q], 0))
    same_core = [list(range(0, blk_count, 2)), list(range(1, blk_count, 2))]
    kv = lax.all_gather(chip_kv, "blk", axis=0, tiled=True, axis_index_groups=same_core)
    scalars = jnp.stack(
        [length, (blk_index - core).astype(jnp.int32), jnp.int32(cache_len)]
    )
    chip_out = attention(scalars, chip_q, kv, tok_rows)
    own_out = lax.dynamic_slice_in_dim(chip_out, core * tok_rows, tok_rows, 0)
    sent_out = lax.dynamic_slice_in_dim(chip_out, (1 - core) * tok_rows, tok_rows, 0)
    got_out = lax.ppermute(sent_out, "blk", pairs)
    attended = jnp.where(
        first, jnp.concatenate([own_out, got_out], 1), jnp.concatenate([got_out, own_out], 1)
    )
    attended, other_gate_up, other_down = lax.optimization_barrier(
        (attended, other_gate_up, other_down)
    )

    residual = inputs[0].astype(jnp.float32) + jnp.dot(
        attended, w_out, preferred_element_type=jnp.float32
    )
    normalized = (
        residual
        * lax.rsqrt(jnp.mean(residual * residual, axis=-1, keepdims=True) + 1e-06)
        * norm_gain
    ).astype(jnp.bfloat16)

    devices = lax.axis_size("req") * blk_count
    capacity = max(2, tok_rows * TOP * 2 // EXPERTS)
    half_cap = -(-((capacity + 1) // 2) // 8) * 8
    flat_ids = route_ids[0].reshape(-1)
    onehot = (flat_ids[:, None] == jnp.arange(EXPERTS, dtype=jnp.int32)[None, :]).astype(jnp.int32)
    slot_index = jnp.sum((jnp.cumsum(onehot, axis=0) - onehot) * onehot, axis=1)
    slot_target = (2 * flat_ids + slot_index % 2) * half_cap + slot_index // 2
    slot_match = slot_target[:, None] == jnp.arange(devices * half_cap, dtype=jnp.int32)[None, :]
    dispatch = jnp.sum(slot_match.reshape(tok_rows, TOP, -1).astype(jnp.float32), axis=1).astype(
        jnp.bfloat16
    )
    combine_weights = jnp.sum(
        jnp.where(slot_match, route_weights[0].reshape(-1)[:, None], 0.0).reshape(
            tok_rows, TOP, -1
        ),
        axis=1,
    )
    outgoing = lax.dot_general(
        dispatch, normalized, (((0,), (0,)), ((), ())), preferred_element_type=jnp.float32
    ).astype(jnp.bfloat16)
    arrived = lax.all_to_all(outgoing, ("req", "blk"), split_axis=0, concat_axis=0, tiled=True)
    mine = half_expert(arrived, w_gate_up[0], w_down[0])
    other = half_expert(arrived, other_gate_up, other_down)
    both = (mine.astype(jnp.float32) + other.astype(jnp.float32)).astype(jnp.bfloat16)
    returned = lax.all_to_all(both, ("req", "blk"), split_axis=0, concat_axis=0, tiled=True)
    expert_sum = jnp.dot(
        combine_weights,
        returned.astype(jnp.float32),
        precision=lax.Precision.HIGHEST,
        preferred_element_type=jnp.float32,
    )
    return (residual + expert_sum).astype(jnp.bfloat16)[None]


def solution(mesh):
    in_specs = (
        P("req", "blk", None),
        P("req", "blk", None),
        P("req", "blk", None),
        P("req", "blk", None),
        P("req", "blk", None),
        P("req"),
        P("req", "blk", None),
        P(),
        P(),
        P("req", "blk", None),
        P("req", "blk", None),
        P(("req", "blk"), None, None),
        P(("req", "blk"), None, None),
    )
    out_specs = P("req", "blk", None)
    return jax.shard_map(local, mesh=mesh, in_specs=in_specs, out_specs=out_specs, check_vma=False)
```

```python
import math

import jax
import jax.numpy as jnp
from jax import lax
from jax.experimental import pallas as pl
from jax.experimental.pallas import tpu as pltpu
from jax.sharding import PartitionSpec as P

D = 2048
HEADS = 16
KV_HEADS = 4
HEAD_DIM = 128
EXPERTS = 64
TOP = 6


CHUNK = 1024


def attn_kernel(s_ref, q_ref, k_ref, v_ref, o_ref):
    group_size = HEADS // KV_HEADS
    tok_rows = q_ref.shape[0]
    rows = tok_rows * group_size
    length = s_ref[0]
    blk = s_ref[1] + pl.program_id(1)
    qb = q_ref[...]
    qs = jnp.concatenate([qb[:, r * HEAD_DIM:(r + 1) * HEAD_DIM] for r in range(group_size)], axis=0)
    qpos = blk * tok_rows + lax.broadcasted_iota(jnp.int32, (rows, 1), 0) % tok_rows
    col = lax.broadcasted_iota(jnp.int32, (1, CHUNK), 1)
    cache_devs = CHUNK // CACHE_ROWS
    span_devs = CHUNK // SPAN_ROWS
    n_cache = (length + CHUNK - 1) // CHUNK
    n_span = (blk * tok_rows + tok_rows - 1) // CHUNK + 1
    factor = math.log2(math.e) / math.sqrt(HEAD_DIM)

    def cache_rows(ref, c):
        return ref[pl.ds(c * cache_devs, cache_devs), pl.ds(0, CACHE_ROWS), :].reshape(CHUNK, HEAD_DIM)

    def span_rows(ref, c):
        return ref[pl.ds(c * span_devs, span_devs), pl.ds(CACHE_ROWS, SPAN_ROWS), :].reshape(CHUNK, HEAD_DIM)

    def scores(k):
        return lax.dot_general(qs, k, (((1,), (1,)), ((), ())), preferred_element_type=jnp.float32)

    def cache_mask(c):
        return (c * CHUNK + col) < length

    def span_mask(c):
        return (c * CHUNK + col) <= qpos

    def step(rows_of, mask_of):
        def body(c, carry):
            m, l, acc = carry
            s = scores(rows_of(k_ref, c))
            if mask_of is not None:
                s = jnp.where(mask_of(c), s, -1e30)
            m_new = jnp.maximum(m, jnp.max(s, axis=-1, keepdims=True))
            alpha = jnp.exp2((m - m_new) * factor)
            p = jnp.exp2((s - m_new) * factor)
            l = alpha * l + jnp.sum(p, axis=-1, keepdims=True)
            acc = alpha * acc + jnp.dot(
                p.astype(jnp.bfloat16), rows_of(v_ref, c), preferred_element_type=jnp.float32
            )
            return m_new, l, acc
        return body

    carry = (
        jnp.full((rows, 1), -1e30, jnp.float32),
        jnp.zeros((rows, 1), jnp.float32),
        jnp.zeros((rows, HEAD_DIM), jnp.float32),
    )
    cache_full = length // CHUNK
    span_full = (blk * tok_rows + 1) // CHUNK
    carry = lax.fori_loop(0, cache_full, step(cache_rows, None), carry)
    carry = lax.fori_loop(cache_full, n_cache, step(cache_rows, cache_mask), carry)
    carry = lax.fori_loop(0, span_full, step(span_rows, None), carry)
    _, l, acc = lax.fori_loop(span_full, n_span, step(span_rows, span_mask), carry)
    out = (acc / l).astype(o_ref.dtype)
    for r in range(group_size):
        o_ref[:, r * HEAD_DIM:(r + 1) * HEAD_DIM] = out[r * tok_rows:(r + 1) * tok_rows]


CACHE_ROWS = 128
SPAN_ROWS = 64


def attention(scalars, queries, kv, tok_rows):
    groups = queries.shape[1] // (HEAD_DIM * HEADS // KV_HEADS)
    halves = queries.shape[0] // tok_rows
    devs, per_dev, _ = kv.shape
    group_cols = HEAD_DIM * HEADS // KV_HEADS
    return pl.pallas_call(
        attn_kernel,
        out_shape=jax.ShapeDtypeStruct(queries.shape, jnp.bfloat16),
        grid=(groups, halves),
        in_specs=[
            pl.BlockSpec(memory_space=pltpu.SMEM),
            pl.BlockSpec((tok_rows, group_cols), lambda g, h: (h, g)),
            pl.BlockSpec((devs, per_dev, HEAD_DIM), lambda g, h: (0, 0, g)),
            pl.BlockSpec((devs, per_dev, HEAD_DIM), lambda g, h: (0, 0, groups + g)),
        ],
        out_specs=pl.BlockSpec((tok_rows, group_cols), lambda g, h: (h, g)),
        compiler_params=pltpu.CompilerParams(
            dimension_semantics=("arbitrary", "arbitrary"), vmem_limit_bytes=40 * 1024 * 1024
        ),
    )(scalars, queries, kv, kv)


def half_expert(arrived, gate_up, down_rows):
    half_width = down_rows.shape[0]
    hidden = jnp.dot(arrived, gate_up.T, preferred_element_type=jnp.float32)
    activated = (jax.nn.silu(hidden[:, :half_width]) * hidden[:, half_width:]).astype(jnp.bfloat16)
    return jnp.dot(activated, down_rows, preferred_element_type=jnp.float32).astype(jnp.bfloat16)


def local(
    queries,
    span_keys,
    span_values,
    cache_keys,
    cache_values,
    lengths,
    inputs,
    w_out,
    norm_gain,
    route_ids,
    route_weights,
    w_gate_up,
    w_down,
):
    tok_rows = queries.shape[1]
    blk_count = lax.axis_size("blk")
    blk_index = lax.axis_index("blk")
    length = lengths[0]
    cache_len = cache_keys.shape[1]
    span_len = span_keys.shape[1]

    pairs = [(b, b ^ 1) for b in range(blk_count)]
    other_gate_up = lax.ppermute(w_gate_up[0], "blk", pairs)
    other_down = lax.ppermute(w_down[0], "blk", pairs)

    core = blk_index % 2
    half_cols = KV_HEADS * HEAD_DIM // 2
    key_rows = jnp.concatenate([cache_keys[0], span_keys[0]], 0)
    value_rows = jnp.concatenate([cache_values[0], span_values[0]], 0)

    def kv_cols(which):
        return jnp.concatenate(
            [
                lax.dynamic_slice_in_dim(key_rows, which * half_cols, half_cols, 1),
                lax.dynamic_slice_in_dim(value_rows, which * half_cols, half_cols, 1),
            ],
            1,
        )

    q_cols = queries.shape[2] // 2
    own_q = lax.dynamic_slice_in_dim(queries[0], core * q_cols, q_cols, 1)
    sent_q = lax.dynamic_slice_in_dim(queries[0], (1 - core) * q_cols, q_cols, 1)
    own_kv = kv_cols(core)
    got_kv, got_q = lax.ppermute((kv_cols(1 - core), sent_q), "blk", pairs)
    first = core == 0
    chip_kv = jnp.where(first, jnp.stack([own_kv, got_kv]), jnp.stack([got_kv, own_kv]))
    chip_q = jnp.where(first, jnp.concatenate([own_q, got_q], 0), jnp.concatenate([got_q, own_q], 0))
    same_core = [list(range(0, blk_count, 2)), list(range(1, blk_count, 2))]
    kv = lax.all_gather(chip_kv, "blk", axis=0, tiled=True, axis_index_groups=same_core)
    scalars = jnp.stack(
        [length, (blk_index - core).astype(jnp.int32), jnp.int32(cache_len)]
    )
    chip_out = attention(scalars, chip_q, kv, tok_rows)
    own_out = lax.dynamic_slice_in_dim(chip_out, core * tok_rows, tok_rows, 0)
    sent_out = lax.dynamic_slice_in_dim(chip_out, (1 - core) * tok_rows, tok_rows, 0)
    got_out = lax.ppermute(sent_out, "blk", pairs)
    attended = jnp.where(
        first, jnp.concatenate([own_out, got_out], 1), jnp.concatenate([got_out, own_out], 1)
    )
    attended, other_gate_up, other_down = lax.optimization_barrier(
        (attended, other_gate_up, other_down)
    )

    residual = inputs[0].astype(jnp.float32) + jnp.dot(
        attended, w_out, preferred_element_type=jnp.float32
    )
    normalized = (
        residual
        * lax.rsqrt(jnp.mean(residual * residual, axis=-1, keepdims=True) + 1e-06)
        * norm_gain
    ).astype(jnp.bfloat16)

    devices = lax.axis_size("req") * blk_count
    capacity = max(2, tok_rows * TOP * 2 // EXPERTS)
    half_cap = -(-((capacity + 1) // 2) // 8) * 8
    flat_ids = route_ids[0].reshape(-1)
    onehot = (flat_ids[:, None] == jnp.arange(EXPERTS, dtype=jnp.int32)[None, :]).astype(jnp.int32)
    slot_index = jnp.sum((jnp.cumsum(onehot, axis=0) - onehot) * onehot, axis=1)
    slot_target = (2 * flat_ids + slot_index % 2) * half_cap + slot_index // 2
    slot_match = slot_target[:, None] == jnp.arange(devices * half_cap, dtype=jnp.int32)[None, :]
    dispatch = jnp.sum(slot_match.reshape(tok_rows, TOP, -1).astype(jnp.float32), axis=1).astype(
        jnp.bfloat16
    )
    combine_weights = jnp.sum(
        jnp.where(slot_match, route_weights[0].reshape(-1)[:, None], 0.0).reshape(
            tok_rows, TOP, -1
        ),
        axis=1,
    )
    outgoing = lax.dot_general(
        dispatch, normalized, (((0,), (0,)), ((), ())), preferred_element_type=jnp.float32
    ).astype(jnp.bfloat16)
    arrived = lax.all_to_all(outgoing, ("req", "blk"), split_axis=0, concat_axis=0, tiled=True)
    mine = half_expert(arrived, w_gate_up[0], w_down[0])
    other = half_expert(arrived, other_gate_up, other_down)
    both = (mine.astype(jnp.float32) + other.astype(jnp.float32)).astype(jnp.bfloat16)
    returned = lax.all_to_all(both, ("req", "blk"), split_axis=0, concat_axis=0, tiled=True)
    expert_sum = jnp.dot(
        combine_weights,
        returned.astype(jnp.float32),
        precision=lax.Precision.HIGHEST,
        preferred_element_type=jnp.float32,
    )
    return (residual + expert_sum).astype(jnp.bfloat16)[None]


def solution(mesh):
    in_specs = (
        P("req", "blk", None),
        P("req", "blk", None),
        P("req", "blk", None),
        P("req", "blk", None),
        P("req", "blk", None),
        P("req"),
        P("req", "blk", None),
        P(),
        P(),
        P("req", "blk", None),
        P("req", "blk", None),
        P(("req", "blk"), None, None),
        P(("req", "blk"), None, None),
    )
    out_specs = P("req", "blk", None)
    return jax.shard_map(local, mesh=mesh, in_specs=in_specs, out_specs=out_specs, check_vma=False)
```

```python
import math

import jax
import jax.numpy as jnp
from jax import lax
from jax.experimental import pallas as pl
from jax.experimental.pallas import tpu as pltpu
from jax.sharding import PartitionSpec as P

D = 2048
HEADS = 16
KV_HEADS = 4
HEAD_DIM = 128
EXPERTS = 64
TOP = 6


CHUNK = 2048


def attn_kernel(s_ref, q_ref, k_ref, v_ref, o_ref):
    group_size = HEADS // KV_HEADS
    tok_rows = q_ref.shape[0]
    rows = tok_rows * group_size
    length = s_ref[0]
    blk = s_ref[1] + pl.program_id(1)
    qb = q_ref[...]
    qs = jnp.concatenate([qb[:, r * HEAD_DIM:(r + 1) * HEAD_DIM] for r in range(group_size)], axis=0)
    qpos = blk * tok_rows + lax.broadcasted_iota(jnp.int32, (rows, 1), 0) % tok_rows
    col = lax.broadcasted_iota(jnp.int32, (1, CHUNK), 1)
    cache_devs = CHUNK // CACHE_ROWS
    span_devs = CHUNK // SPAN_ROWS
    n_cache = (length + CHUNK - 1) // CHUNK
    n_span = (blk * tok_rows + tok_rows - 1) // CHUNK + 1
    factor = math.log2(math.e) / math.sqrt(HEAD_DIM)

    def cache_rows(ref, c):
        return ref[pl.ds(c * cache_devs, cache_devs), pl.ds(0, CACHE_ROWS), :].reshape(CHUNK, HEAD_DIM)

    def span_rows(ref, c):
        return ref[pl.ds(c * span_devs, span_devs), pl.ds(CACHE_ROWS, SPAN_ROWS), :].reshape(CHUNK, HEAD_DIM)

    def scores(k):
        return lax.dot_general(qs, k, (((1,), (1,)), ((), ())), preferred_element_type=jnp.float32)

    def cache_mask(c):
        return (c * CHUNK + col) < length

    def span_mask(c):
        return (c * CHUNK + col) <= qpos

    def step(rows_of, mask_of):
        def body(c, carry):
            m, l, acc = carry
            s = scores(rows_of(k_ref, c))
            if mask_of is not None:
                s = jnp.where(mask_of(c), s, -1e30)
            m_new = jnp.maximum(m, jnp.max(s, axis=-1, keepdims=True))
            alpha = jnp.exp2((m - m_new) * factor)
            p = jnp.exp2((s - m_new) * factor)
            l = alpha * l + jnp.sum(p, axis=-1, keepdims=True)
            acc = alpha * acc + jnp.dot(
                p.astype(jnp.bfloat16), rows_of(v_ref, c), preferred_element_type=jnp.float32
            )
            return m_new, l, acc
        return body

    carry = (
        jnp.full((rows, 1), -1e30, jnp.float32),
        jnp.zeros((rows, 1), jnp.float32),
        jnp.zeros((rows, HEAD_DIM), jnp.float32),
    )
    cache_full = length // CHUNK
    span_full = (blk * tok_rows + 1) // CHUNK
    carry = lax.fori_loop(0, cache_full, step(cache_rows, None), carry)
    carry = lax.fori_loop(cache_full, n_cache, step(cache_rows, cache_mask), carry)
    carry = lax.fori_loop(0, span_full, step(span_rows, None), carry)
    _, l, acc = lax.fori_loop(span_full, n_span, step(span_rows, span_mask), carry)
    out = (acc / l).astype(o_ref.dtype)
    for r in range(group_size):
        o_ref[:, r * HEAD_DIM:(r + 1) * HEAD_DIM] = out[r * tok_rows:(r + 1) * tok_rows]


CACHE_ROWS = 128
SPAN_ROWS = 64


def attention(scalars, queries, kv, tok_rows):
    groups = queries.shape[1] // (HEAD_DIM * HEADS // KV_HEADS)
    halves = queries.shape[0] // tok_rows
    devs, per_dev, _ = kv.shape
    group_cols = HEAD_DIM * HEADS // KV_HEADS
    return pl.pallas_call(
        attn_kernel,
        out_shape=jax.ShapeDtypeStruct(queries.shape, jnp.bfloat16),
        grid=(groups, halves),
        in_specs=[
            pl.BlockSpec(memory_space=pltpu.SMEM),
            pl.BlockSpec((tok_rows, group_cols), lambda g, h: (h, g)),
            pl.BlockSpec((devs, per_dev, HEAD_DIM), lambda g, h: (0, 0, g)),
            pl.BlockSpec((devs, per_dev, HEAD_DIM), lambda g, h: (0, 0, groups + g)),
        ],
        out_specs=pl.BlockSpec((tok_rows, group_cols), lambda g, h: (h, g)),
        compiler_params=pltpu.CompilerParams(
            dimension_semantics=("arbitrary", "arbitrary"), vmem_limit_bytes=40 * 1024 * 1024
        ),
    )(scalars, queries, kv, kv)


def half_expert(arrived, gate_up, down_rows):
    half_width = down_rows.shape[0]
    hidden = jnp.dot(arrived, gate_up.T, preferred_element_type=jnp.float32)
    activated = (jax.nn.silu(hidden[:, :half_width]) * hidden[:, half_width:]).astype(jnp.bfloat16)
    return jnp.dot(activated, down_rows, preferred_element_type=jnp.float32).astype(jnp.bfloat16)


def local(
    queries,
    span_keys,
    span_values,
    cache_keys,
    cache_values,
    lengths,
    inputs,
    w_out,
    norm_gain,
    route_ids,
    route_weights,
    w_gate_up,
    w_down,
):
    tok_rows = queries.shape[1]
    blk_count = lax.axis_size("blk")
    blk_index = lax.axis_index("blk")
    length = lengths[0]
    cache_len = cache_keys.shape[1]
    span_len = span_keys.shape[1]

    pairs = [(b, b ^ 1) for b in range(blk_count)]
    other_gate_up = lax.ppermute(w_gate_up[0], "blk", pairs)
    other_down = lax.ppermute(w_down[0], "blk", pairs)

    core = blk_index % 2
    half_cols = KV_HEADS * HEAD_DIM // 2
    key_rows = jnp.concatenate([cache_keys[0], span_keys[0]], 0)
    value_rows = jnp.concatenate([cache_values[0], span_values[0]], 0)

    def kv_cols(which):
        return jnp.concatenate(
            [
                lax.dynamic_slice_in_dim(key_rows, which * half_cols, half_cols, 1),
                lax.dynamic_slice_in_dim(value_rows, which * half_cols, half_cols, 1),
            ],
            1,
        )

    q_cols = queries.shape[2] // 2
    own_q = lax.dynamic_slice_in_dim(queries[0], core * q_cols, q_cols, 1)
    sent_q = lax.dynamic_slice_in_dim(queries[0], (1 - core) * q_cols, q_cols, 1)
    own_kv = kv_cols(core)
    got_kv, got_q = lax.ppermute((kv_cols(1 - core), sent_q), "blk", pairs)
    first = core == 0
    chip_kv = jnp.where(first, jnp.stack([own_kv, got_kv]), jnp.stack([got_kv, own_kv]))
    chip_q = jnp.where(first, jnp.concatenate([own_q, got_q], 0), jnp.concatenate([got_q, own_q], 0))
    same_core = [list(range(0, blk_count, 2)), list(range(1, blk_count, 2))]
    kv = lax.all_gather(chip_kv, "blk", axis=0, tiled=True, axis_index_groups=same_core)
    scalars = jnp.stack(
        [length, (blk_index - core).astype(jnp.int32), jnp.int32(cache_len)]
    )
    chip_out = attention(scalars, chip_q, kv, tok_rows)
    own_out = lax.dynamic_slice_in_dim(chip_out, core * tok_rows, tok_rows, 0)
    sent_out = lax.dynamic_slice_in_dim(chip_out, (1 - core) * tok_rows, tok_rows, 0)
    got_out = lax.ppermute(sent_out, "blk", pairs)
    attended = jnp.where(
        first, jnp.concatenate([own_out, got_out], 1), jnp.concatenate([got_out, own_out], 1)
    )
    attended, other_gate_up, other_down = lax.optimization_barrier(
        (attended, other_gate_up, other_down)
    )

    residual = inputs[0].astype(jnp.float32) + jnp.dot(
        attended, w_out, preferred_element_type=jnp.float32
    )
    normalized = (
        residual
        * lax.rsqrt(jnp.mean(residual * residual, axis=-1, keepdims=True) + 1e-06)
        * norm_gain
    ).astype(jnp.bfloat16)

    devices = lax.axis_size("req") * blk_count
    capacity = max(2, tok_rows * TOP * 2 // EXPERTS)
    half_cap = -(-((capacity + 1) // 2) // 8) * 8
    flat_ids = route_ids[0].reshape(-1)
    onehot = (flat_ids[:, None] == jnp.arange(EXPERTS, dtype=jnp.int32)[None, :]).astype(jnp.int32)
    slot_index = jnp.sum((jnp.cumsum(onehot, axis=0) - onehot) * onehot, axis=1)
    slot_target = (2 * flat_ids + slot_index % 2) * half_cap + slot_index // 2
    slot_match = slot_target[:, None] == jnp.arange(devices * half_cap, dtype=jnp.int32)[None, :]
    dispatch = jnp.sum(slot_match.reshape(tok_rows, TOP, -1).astype(jnp.float32), axis=1).astype(
        jnp.bfloat16
    )
    combine_weights = jnp.sum(
        jnp.where(slot_match, route_weights[0].reshape(-1)[:, None], 0.0).reshape(
            tok_rows, TOP, -1
        ),
        axis=1,
    )
    outgoing = lax.dot_general(
        dispatch, normalized, (((0,), (0,)), ((), ())), preferred_element_type=jnp.float32
    ).astype(jnp.bfloat16)
    arrived = lax.all_to_all(outgoing, ("req", "blk"), split_axis=0, concat_axis=0, tiled=True)
    mine = half_expert(arrived, w_gate_up[0], w_down[0])
    other = half_expert(arrived, other_gate_up, other_down)
    both = (mine.astype(jnp.float32) + other.astype(jnp.float32)).astype(jnp.bfloat16)
    returned = lax.all_to_all(both, ("req", "blk"), split_axis=0, concat_axis=0, tiled=True)
    expert_sum = jnp.dot(
        combine_weights,
        returned.astype(jnp.float32),
        precision=lax.Precision.HIGHEST,
        preferred_element_type=jnp.float32,
    )
    return (residual + expert_sum).astype(jnp.bfloat16)[None]


def solution(mesh):
    in_specs = (
        P("req", "blk", None),
        P("req", "blk", None),
        P("req", "blk", None),
        P("req", "blk", None),
        P("req", "blk", None),
        P("req"),
        P("req", "blk", None),
        P(),
        P(),
        P("req", "blk", None),
        P("req", "blk", None),
        P(("req", "blk"), None, None),
        P(("req", "blk"), None, None),
    )
    out_specs = P("req", "blk", None)
    return jax.shard_map(local, mesh=mesh, in_specs=in_specs, out_specs=out_specs, check_vma=False)
```

```python
import math

import jax
import jax.numpy as jnp
from jax import lax
from jax.experimental import pallas as pl
from jax.experimental.pallas import tpu as pltpu
from jax.sharding import PartitionSpec as P

D = 2048
HEADS = 16
KV_HEADS = 4
HEAD_DIM = 128
EXPERTS = 64
TOP = 6


CHUNK = 2048


def attn_kernel(s_ref, q_ref, k_ref, v_ref, o_ref):
    group_size = HEADS // KV_HEADS
    tok_rows = q_ref.shape[0]
    rows = tok_rows * group_size
    length = s_ref[0]
    blk = s_ref[1] // 2
    qb = q_ref[...]
    qs = jnp.concatenate([qb[:, r * HEAD_DIM:(r + 1) * HEAD_DIM] for r in range(group_size)], axis=0)
    qpos = blk * tok_rows + lax.broadcasted_iota(jnp.int32, (rows, 1), 0) % tok_rows
    col = lax.broadcasted_iota(jnp.int32, (1, CHUNK), 1)
    cache_devs = CHUNK // CACHE_ROWS
    span_devs = CHUNK // SPAN_ROWS
    n_cache = (length + CHUNK - 1) // CHUNK
    n_span = (blk * tok_rows + tok_rows - 1) // CHUNK + 1
    factor = math.log2(math.e) / math.sqrt(HEAD_DIM)

    def cache_rows(ref, c):
        return ref[pl.ds(c * cache_devs, cache_devs), pl.ds(0, CACHE_ROWS), :].reshape(CHUNK, HEAD_DIM)

    def span_rows(ref, c):
        return ref[pl.ds(c * span_devs, span_devs), pl.ds(CACHE_ROWS, SPAN_ROWS), :].reshape(CHUNK, HEAD_DIM)

    def scores(k):
        return lax.dot_general(qs, k, (((1,), (1,)), ((), ())), preferred_element_type=jnp.float32)

    def cache_mask(c):
        return (c * CHUNK + col) < length

    def span_mask(c):
        return (c * CHUNK + col) <= qpos

    def step(rows_of, mask_of):
        def body(c, carry):
            m, l, acc = carry
            s = scores(rows_of(k_ref, c))
            if mask_of is not None:
                s = jnp.where(mask_of(c), s, -1e30)
            m_new = jnp.maximum(m, jnp.max(s, axis=-1, keepdims=True))
            alpha = jnp.exp2((m - m_new) * factor)
            p = jnp.exp2((s - m_new) * factor)
            l = alpha * l + jnp.sum(p, axis=-1, keepdims=True)
            acc = alpha * acc + jnp.dot(
                p.astype(jnp.bfloat16), rows_of(v_ref, c), preferred_element_type=jnp.float32
            )
            return m_new, l, acc
        return body

    carry = (
        jnp.full((rows, 1), -1e30, jnp.float32),
        jnp.zeros((rows, 1), jnp.float32),
        jnp.zeros((rows, HEAD_DIM), jnp.float32),
    )
    cache_full = length // CHUNK
    span_full = (blk * tok_rows + 1) // CHUNK
    carry = lax.fori_loop(0, cache_full, step(cache_rows, None), carry)
    carry = lax.fori_loop(cache_full, n_cache, step(cache_rows, cache_mask), carry)
    carry = lax.fori_loop(0, span_full, step(span_rows, None), carry)
    _, l, acc = lax.fori_loop(span_full, n_span, step(span_rows, span_mask), carry)
    out = (acc / l).astype(o_ref.dtype)
    for r in range(group_size):
        o_ref[:, r * HEAD_DIM:(r + 1) * HEAD_DIM] = out[r * tok_rows:(r + 1) * tok_rows]


CACHE_ROWS = 128
SPAN_ROWS = 64


def attention(scalars, queries, kv):
    groups = queries.shape[1] // (HEAD_DIM * HEADS // KV_HEADS)
    devs, per_dev, _ = kv.shape
    group_cols = HEAD_DIM * HEADS // KV_HEADS
    chip_rows = queries.shape[0]
    return pl.pallas_call(
        attn_kernel,
        out_shape=jax.ShapeDtypeStruct(queries.shape, jnp.bfloat16),
        grid=(groups,),
        in_specs=[
            pl.BlockSpec(memory_space=pltpu.SMEM),
            pl.BlockSpec((chip_rows, group_cols), lambda g: (0, g)),
            pl.BlockSpec((devs, per_dev, HEAD_DIM), lambda g: (0, 0, g)),
            pl.BlockSpec((devs, per_dev, HEAD_DIM), lambda g: (0, 0, groups + g)),
        ],
        out_specs=pl.BlockSpec((chip_rows, group_cols), lambda g: (0, g)),
        compiler_params=pltpu.CompilerParams(
            dimension_semantics=("arbitrary",), vmem_limit_bytes=48 * 1024 * 1024
        ),
    )(scalars, queries, kv, kv)


def half_expert(arrived, gate_up, down_rows):
    half_width = down_rows.shape[0]
    hidden = jnp.dot(arrived, gate_up.T, preferred_element_type=jnp.float32)
    activated = (jax.nn.silu(hidden[:, :half_width]) * hidden[:, half_width:]).astype(jnp.bfloat16)
    return jnp.dot(activated, down_rows, preferred_element_type=jnp.float32).astype(jnp.bfloat16)


def local(
    queries,
    span_keys,
    span_values,
    cache_keys,
    cache_values,
    lengths,
    inputs,
    w_out,
    norm_gain,
    route_ids,
    route_weights,
    w_gate_up,
    w_down,
):
    tok_rows = queries.shape[1]
    blk_count = lax.axis_size("blk")
    blk_index = lax.axis_index("blk")
    length = lengths[0]
    cache_len = cache_keys.shape[1]
    span_len = span_keys.shape[1]

    pairs = [(b, b ^ 1) for b in range(blk_count)]
    other_gate_up = lax.ppermute(w_gate_up[0], "blk", pairs)
    other_down = lax.ppermute(w_down[0], "blk", pairs)

    core = blk_index % 2
    half_cols = KV_HEADS * HEAD_DIM // 2
    key_rows = jnp.concatenate([cache_keys[0], span_keys[0]], 0)
    value_rows = jnp.concatenate([cache_values[0], span_values[0]], 0)

    def kv_cols(which):
        return jnp.concatenate(
            [
                lax.dynamic_slice_in_dim(key_rows, which * half_cols, half_cols, 1),
                lax.dynamic_slice_in_dim(value_rows, which * half_cols, half_cols, 1),
            ],
            1,
        )

    q_cols = queries.shape[2] // 2
    own_q = lax.dynamic_slice_in_dim(queries[0], core * q_cols, q_cols, 1)
    sent_q = lax.dynamic_slice_in_dim(queries[0], (1 - core) * q_cols, q_cols, 1)
    own_kv = kv_cols(core)
    got_kv, got_q = lax.ppermute((kv_cols(1 - core), sent_q), "blk", pairs)
    first = core == 0
    chip_kv = jnp.where(first, jnp.stack([own_kv, got_kv]), jnp.stack([got_kv, own_kv]))
    chip_q = jnp.where(first, jnp.concatenate([own_q, got_q], 0), jnp.concatenate([got_q, own_q], 0))
    same_core = [list(range(0, blk_count, 2)), list(range(1, blk_count, 2))]
    kv = lax.all_gather(chip_kv, "blk", axis=0, tiled=True, axis_index_groups=same_core)
    scalars = jnp.stack(
        [length, (blk_index - core).astype(jnp.int32), jnp.int32(cache_len)]
    )
    chip_out = attention(scalars, chip_q, kv)
    own_out = lax.dynamic_slice_in_dim(chip_out, core * tok_rows, tok_rows, 0)
    sent_out = lax.dynamic_slice_in_dim(chip_out, (1 - core) * tok_rows, tok_rows, 0)
    got_out = lax.ppermute(sent_out, "blk", pairs)
    attended = jnp.where(
        first, jnp.concatenate([own_out, got_out], 1), jnp.concatenate([got_out, own_out], 1)
    )
    attended, other_gate_up, other_down = lax.optimization_barrier(
        (attended, other_gate_up, other_down)
    )

    residual = inputs[0].astype(jnp.float32) + jnp.dot(
        attended, w_out, preferred_element_type=jnp.float32
    )
    normalized = (
        residual
        * lax.rsqrt(jnp.mean(residual * residual, axis=-1, keepdims=True) + 1e-06)
        * norm_gain
    ).astype(jnp.bfloat16)

    devices = lax.axis_size("req") * blk_count
    capacity = max(2, tok_rows * TOP * 2 // EXPERTS)
    half_cap = -(-((capacity + 1) // 2) // 8) * 8
    flat_ids = route_ids[0].reshape(-1)
    onehot = (flat_ids[:, None] == jnp.arange(EXPERTS, dtype=jnp.int32)[None, :]).astype(jnp.int32)
    slot_index = jnp.sum((jnp.cumsum(onehot, axis=0) - onehot) * onehot, axis=1)
    slot_target = (2 * flat_ids + slot_index % 2) * half_cap + slot_index // 2
    slot_match = slot_target[:, None] == jnp.arange(devices * half_cap, dtype=jnp.int32)[None, :]
    dispatch = jnp.sum(slot_match.reshape(tok_rows, TOP, -1).astype(jnp.float32), axis=1).astype(
        jnp.bfloat16
    )
    combine_weights = jnp.sum(
        jnp.where(slot_match, route_weights[0].reshape(-1)[:, None], 0.0).reshape(
            tok_rows, TOP, -1
        ),
        axis=1,
    )
    outgoing = lax.dot_general(
        dispatch, normalized, (((0,), (0,)), ((), ())), preferred_element_type=jnp.float32
    ).astype(jnp.bfloat16)
    arrived = lax.all_to_all(outgoing, ("req", "blk"), split_axis=0, concat_axis=0, tiled=True)
    mine = half_expert(arrived, w_gate_up[0], w_down[0])
    other = half_expert(arrived, other_gate_up, other_down)
    both = (mine.astype(jnp.float32) + other.astype(jnp.float32)).astype(jnp.bfloat16)
    returned = lax.all_to_all(both, ("req", "blk"), split_axis=0, concat_axis=0, tiled=True)
    expert_sum = jnp.dot(
        combine_weights,
        returned.astype(jnp.float32),
        precision=lax.Precision.HIGHEST,
        preferred_element_type=jnp.float32,
    )
    return (residual + expert_sum).astype(jnp.bfloat16)[None]


def solution(mesh):
    in_specs = (
        P("req", "blk", None),
        P("req", "blk", None),
        P("req", "blk", None),
        P("req", "blk", None),
        P("req", "blk", None),
        P("req"),
        P("req", "blk", None),
        P(),
        P(),
        P("req", "blk", None),
        P("req", "blk", None),
        P(("req", "blk"), None, None),
        P(("req", "blk"), None, None),
    )
    out_specs = P("req", "blk", None)
    return jax.shard_map(local, mesh=mesh, in_specs=in_specs, out_specs=out_specs, check_vma=False)
```

```python
import math

import jax
import jax.numpy as jnp
from jax import lax
from jax.experimental import pallas as pl
from jax.experimental.pallas import tpu as pltpu
from jax.sharding import PartitionSpec as P

D = 2048
HEADS = 16
KV_HEADS = 4
HEAD_DIM = 128
EXPERTS = 64
TOP = 6


CHUNK = 2048


def attn_kernel(s_ref, q_ref, k_ref, v_ref, o_ref):
    group_size = HEADS // KV_HEADS
    tok_rows = q_ref.shape[0]
    rows = tok_rows * group_size
    length = s_ref[0]
    blk = s_ref[1] + pl.program_id(1)
    qb = q_ref[...]
    qs = jnp.concatenate([qb[:, r * HEAD_DIM:(r + 1) * HEAD_DIM] for r in range(group_size)], axis=0)
    qpos = blk * tok_rows + lax.broadcasted_iota(jnp.int32, (rows, 1), 0) % tok_rows
    col = lax.broadcasted_iota(jnp.int32, (1, CHUNK), 1)
    cache_devs = CHUNK // CACHE_ROWS
    span_devs = CHUNK // SPAN_ROWS
    n_cache = (length + CHUNK - 1) // CHUNK
    n_span = (blk * tok_rows + tok_rows - 1) // CHUNK + 1
    factor = math.log2(math.e) / math.sqrt(HEAD_DIM)

    def cache_rows(ref, c):
        return ref[pl.ds(c * cache_devs, cache_devs), pl.ds(0, CACHE_ROWS), :].reshape(CHUNK, HEAD_DIM)

    def span_rows(ref, c):
        return ref[pl.ds(c * span_devs, span_devs), pl.ds(CACHE_ROWS, SPAN_ROWS), :].reshape(CHUNK, HEAD_DIM)

    def scores(k):
        return lax.dot_general(qs, k, (((1,), (1,)), ((), ())), preferred_element_type=jnp.float32)

    def cache_mask(c):
        return (c * CHUNK + col) < length

    def span_mask(c):
        return (c * CHUNK + col) <= qpos

    def step(rows_of, mask_of):
        def body(c, carry):
            m, l, acc = carry
            s = scores(rows_of(k_ref, c))
            if mask_of is not None:
                s = jnp.where(mask_of(c), s, -1e30)
            m_new = jnp.maximum(m, jnp.max(s, axis=-1, keepdims=True))
            alpha = jnp.exp2((m - m_new) * factor)
            p = jnp.exp2((s - m_new) * factor)
            l = alpha * l + jnp.sum(p, axis=-1, keepdims=True)
            acc = alpha * acc + jnp.dot(
                p.astype(jnp.bfloat16), rows_of(v_ref, c), preferred_element_type=jnp.float32
            )
            return m_new, l, acc
        return body

    carry = (
        jnp.full((rows, 1), -1e30, jnp.float32),
        jnp.zeros((rows, 1), jnp.float32),
        jnp.zeros((rows, HEAD_DIM), jnp.float32),
    )
    cache_full = length // CHUNK
    span_full = (blk * tok_rows + 1) // CHUNK
    carry = lax.fori_loop(0, cache_full, step(cache_rows, None), carry)
    carry = lax.fori_loop(cache_full, n_cache, step(cache_rows, cache_mask), carry)
    carry = lax.fori_loop(0, span_full, step(span_rows, None), carry)
    _, l, acc = lax.fori_loop(span_full, n_span, step(span_rows, span_mask), carry)
    out = (acc / l).astype(o_ref.dtype)
    for r in range(group_size):
        o_ref[:, r * HEAD_DIM:(r + 1) * HEAD_DIM] = out[r * tok_rows:(r + 1) * tok_rows]


CACHE_ROWS = 128
SPAN_ROWS = 64


def attention(scalars, queries, kv, tok_rows):
    groups = queries.shape[1] // (HEAD_DIM * HEADS // KV_HEADS)
    halves = queries.shape[0] // tok_rows
    devs, per_dev, _ = kv.shape
    group_cols = HEAD_DIM * HEADS // KV_HEADS
    return pl.pallas_call(
        attn_kernel,
        out_shape=jax.ShapeDtypeStruct(queries.shape, jnp.bfloat16),
        grid=(groups, halves),
        in_specs=[
            pl.BlockSpec(memory_space=pltpu.SMEM),
            pl.BlockSpec((tok_rows, group_cols), lambda g, h: (h, g)),
            pl.BlockSpec((devs, per_dev, HEAD_DIM), lambda g, h: (0, 0, g)),
            pl.BlockSpec((devs, per_dev, HEAD_DIM), lambda g, h: (0, 0, groups + g)),
        ],
        out_specs=pl.BlockSpec((tok_rows, group_cols), lambda g, h: (h, g)),
        compiler_params=pltpu.CompilerParams(
            dimension_semantics=("arbitrary", "arbitrary"), vmem_limit_bytes=40 * 1024 * 1024
        ),
    )(scalars, queries, kv, kv)


def half_expert(arrived, gate_up, down_rows):
    half_width = down_rows.shape[0]
    hidden = jnp.dot(arrived, gate_up.T, preferred_element_type=jnp.float32)
    activated = (jax.nn.silu(hidden[:, :half_width]) * hidden[:, half_width:]).astype(jnp.bfloat16)
    return jnp.dot(activated, down_rows, preferred_element_type=jnp.float32).astype(jnp.bfloat16)


def local(
    queries,
    span_keys,
    span_values,
    cache_keys,
    cache_values,
    lengths,
    inputs,
    w_out,
    norm_gain,
    route_ids,
    route_weights,
    w_gate_up,
    w_down,
):
    tok_rows = queries.shape[1]
    blk_count = lax.axis_size("blk")
    blk_index = lax.axis_index("blk")
    length = lengths[0]
    cache_len = cache_keys.shape[1]
    span_len = span_keys.shape[1]

    pairs = [(b, b ^ 1) for b in range(blk_count)]

    core = blk_index % 2
    half_cols = KV_HEADS * HEAD_DIM // 2
    key_rows = jnp.concatenate([cache_keys[0], span_keys[0]], 0)
    value_rows = jnp.concatenate([cache_values[0], span_values[0]], 0)

    def kv_cols(which):
        return jnp.concatenate(
            [
                lax.dynamic_slice_in_dim(key_rows, which * half_cols, half_cols, 1),
                lax.dynamic_slice_in_dim(value_rows, which * half_cols, half_cols, 1),
            ],
            1,
        )

    q_cols = queries.shape[2] // 2
    own_q = lax.dynamic_slice_in_dim(queries[0], core * q_cols, q_cols, 1)
    sent_q = lax.dynamic_slice_in_dim(queries[0], (1 - core) * q_cols, q_cols, 1)
    own_kv = kv_cols(core)
    got_kv, got_q = lax.ppermute((kv_cols(1 - core), sent_q), "blk", pairs)
    first = core == 0
    chip_kv = jnp.where(first, jnp.stack([own_kv, got_kv]), jnp.stack([got_kv, own_kv]))
    chip_q = jnp.where(first, jnp.concatenate([own_q, got_q], 0), jnp.concatenate([got_q, own_q], 0))
    same_core = [list(range(0, blk_count, 2)), list(range(1, blk_count, 2))]
    kv = lax.all_gather(chip_kv, "blk", axis=0, tiled=True, axis_index_groups=same_core)
    kv, chip_q, own_gate_up, own_down = lax.optimization_barrier(
        (kv, chip_q, w_gate_up[0], w_down[0])
    )
    other_gate_up = lax.ppermute(own_gate_up, "blk", pairs)
    other_down = lax.ppermute(own_down, "blk", pairs)
    scalars = jnp.stack(
        [length, (blk_index - core).astype(jnp.int32), jnp.int32(cache_len)]
    )
    chip_out = attention(scalars, chip_q, kv, tok_rows)
    own_out = lax.dynamic_slice_in_dim(chip_out, core * tok_rows, tok_rows, 0)
    sent_out = lax.dynamic_slice_in_dim(chip_out, (1 - core) * tok_rows, tok_rows, 0)
    got_out = lax.ppermute(sent_out, "blk", pairs)
    attended = jnp.where(
        first, jnp.concatenate([own_out, got_out], 1), jnp.concatenate([got_out, own_out], 1)
    )
    attended, other_gate_up, other_down = lax.optimization_barrier(
        (attended, other_gate_up, other_down)
    )

    residual = inputs[0].astype(jnp.float32) + jnp.dot(
        attended, w_out, preferred_element_type=jnp.float32
    )
    normalized = (
        residual
        * lax.rsqrt(jnp.mean(residual * residual, axis=-1, keepdims=True) + 1e-06)
        * norm_gain
    ).astype(jnp.bfloat16)

    devices = lax.axis_size("req") * blk_count
    capacity = max(2, tok_rows * TOP * 2 // EXPERTS)
    half_cap = -(-((capacity + 1) // 2) // 8) * 8
    flat_ids = route_ids[0].reshape(-1)
    onehot = (flat_ids[:, None] == jnp.arange(EXPERTS, dtype=jnp.int32)[None, :]).astype(jnp.int32)
    slot_index = jnp.sum((jnp.cumsum(onehot, axis=0) - onehot) * onehot, axis=1)
    slot_target = (2 * flat_ids + slot_index % 2) * half_cap + slot_index // 2
    slot_match = slot_target[:, None] == jnp.arange(devices * half_cap, dtype=jnp.int32)[None, :]
    dispatch = jnp.sum(slot_match.reshape(tok_rows, TOP, -1).astype(jnp.float32), axis=1).astype(
        jnp.bfloat16
    )
    combine_weights = jnp.sum(
        jnp.where(slot_match, route_weights[0].reshape(-1)[:, None], 0.0).reshape(
            tok_rows, TOP, -1
        ),
        axis=1,
    )
    outgoing = lax.dot_general(
        dispatch, normalized, (((0,), (0,)), ((), ())), preferred_element_type=jnp.float32
    ).astype(jnp.bfloat16)
    arrived = lax.all_to_all(outgoing, ("req", "blk"), split_axis=0, concat_axis=0, tiled=True)
    mine = half_expert(arrived, w_gate_up[0], w_down[0])
    other = half_expert(arrived, other_gate_up, other_down)
    both = (mine.astype(jnp.float32) + other.astype(jnp.float32)).astype(jnp.bfloat16)
    returned = lax.all_to_all(both, ("req", "blk"), split_axis=0, concat_axis=0, tiled=True)
    expert_sum = jnp.dot(
        combine_weights,
        returned.astype(jnp.float32),
        precision=lax.Precision.HIGHEST,
        preferred_element_type=jnp.float32,
    )
    return (residual + expert_sum).astype(jnp.bfloat16)[None]


def solution(mesh):
    in_specs = (
        P("req", "blk", None),
        P("req", "blk", None),
        P("req", "blk", None),
        P("req", "blk", None),
        P("req", "blk", None),
        P("req"),
        P("req", "blk", None),
        P(),
        P(),
        P("req", "blk", None),
        P("req", "blk", None),
        P(("req", "blk"), None, None),
        P(("req", "blk"), None, None),
    )
    out_specs = P("req", "blk", None)
    return jax.shard_map(local, mesh=mesh, in_specs=in_specs, out_specs=out_specs, check_vma=False)
```

```python
import math

import jax
import jax.numpy as jnp
from jax import lax
from jax.experimental import pallas as pl
from jax.experimental.pallas import tpu as pltpu
from jax.sharding import PartitionSpec as P

D = 2048
HEADS = 16
KV_HEADS = 4
HEAD_DIM = 128
EXPERTS = 64
TOP = 6


CHUNK = 2048


def attn_kernel(s_ref, q_ref, k_ref, v_ref, o_ref):
    group_size = HEADS // KV_HEADS
    tok_rows = q_ref.shape[0]
    rows = tok_rows * group_size
    length = s_ref[0]
    blk = s_ref[1] + pl.program_id(1)
    qb = q_ref[...]
    qs = jnp.concatenate([qb[:, r * HEAD_DIM:(r + 1) * HEAD_DIM] for r in range(group_size)], axis=0)
    qpos = blk * tok_rows + lax.broadcasted_iota(jnp.int32, (rows, 1), 0) % tok_rows
    col = lax.broadcasted_iota(jnp.int32, (1, CHUNK), 1)
    cache_devs = CHUNK // CACHE_ROWS
    span_devs = CHUNK // SPAN_ROWS
    n_cache = (length + CHUNK - 1) // CHUNK
    n_span = (blk * tok_rows + tok_rows - 1) // CHUNK + 1
    factor = math.log2(math.e) / math.sqrt(HEAD_DIM)

    def cache_rows(ref, c):
        return ref[pl.ds(c * cache_devs, cache_devs), pl.ds(0, CACHE_ROWS), :].reshape(CHUNK, HEAD_DIM)

    def span_rows(ref, c):
        return ref[pl.ds(c * span_devs, span_devs), pl.ds(CACHE_ROWS, SPAN_ROWS), :].reshape(CHUNK, HEAD_DIM)

    def scores(k):
        return lax.dot_general(qs, k, (((1,), (1,)), ((), ())), preferred_element_type=jnp.float32)

    def cache_mask(c):
        return (c * CHUNK + col) < length

    def span_mask(c):
        return (c * CHUNK + col) <= qpos

    def step(rows_of, mask_of):
        def body(c, carry):
            m, l, acc = carry
            s = scores(rows_of(k_ref, c))
            if mask_of is not None:
                s = jnp.where(mask_of(c), s, -1e30)
            m_new = jnp.maximum(m, jnp.max(s, axis=-1, keepdims=True))
            alpha = jnp.exp2((m - m_new) * factor)
            p = jnp.exp2((s - m_new) * factor)
            l = alpha * l + jnp.sum(p, axis=-1, keepdims=True)
            acc = alpha * acc + jnp.dot(
                p.astype(jnp.bfloat16), rows_of(v_ref, c), preferred_element_type=jnp.float32
            )
            return m_new, l, acc
        return body

    carry = (
        jnp.full((rows, 1), -1e30, jnp.float32),
        jnp.zeros((rows, 1), jnp.float32),
        jnp.zeros((rows, HEAD_DIM), jnp.float32),
    )
    cache_full = length // CHUNK
    span_full = (blk * tok_rows + 1) // CHUNK
    carry = lax.fori_loop(0, cache_full, step(cache_rows, None), carry)
    carry = lax.fori_loop(cache_full, n_cache, step(cache_rows, cache_mask), carry)
    carry = lax.fori_loop(0, span_full, step(span_rows, None), carry)
    _, l, acc = lax.fori_loop(span_full, n_span, step(span_rows, span_mask), carry)
    out = (acc / l).astype(o_ref.dtype)
    for r in range(group_size):
        o_ref[:, r * HEAD_DIM:(r + 1) * HEAD_DIM] = out[r * tok_rows:(r + 1) * tok_rows]


CACHE_ROWS = 128
SPAN_ROWS = 64


def attention(scalars, queries, kv, tok_rows):
    groups = queries.shape[1] // (HEAD_DIM * HEADS // KV_HEADS)
    halves = queries.shape[0] // tok_rows
    devs, per_dev, _ = kv.shape
    group_cols = HEAD_DIM * HEADS // KV_HEADS
    return pl.pallas_call(
        attn_kernel,
        out_shape=jax.ShapeDtypeStruct(queries.shape, jnp.bfloat16),
        grid=(groups, halves),
        in_specs=[
            pl.BlockSpec(memory_space=pltpu.SMEM),
            pl.BlockSpec((tok_rows, group_cols), lambda g, h: (h, g)),
            pl.BlockSpec((devs, per_dev, HEAD_DIM), lambda g, h: (0, 0, g)),
            pl.BlockSpec((devs, per_dev, HEAD_DIM), lambda g, h: (0, 0, groups + g)),
        ],
        out_specs=pl.BlockSpec((tok_rows, group_cols), lambda g, h: (h, g)),
        compiler_params=pltpu.CompilerParams(
            dimension_semantics=("arbitrary", "arbitrary"), vmem_limit_bytes=40 * 1024 * 1024
        ),
    )(scalars, queries, kv, kv)


def half_expert(arrived, gate_up, down_rows):
    half_width = down_rows.shape[0]
    hidden = jnp.dot(arrived, gate_up.T, preferred_element_type=jnp.float32)
    activated = (jax.nn.silu(hidden[:, :half_width]) * hidden[:, half_width:]).astype(jnp.bfloat16)
    return jnp.dot(activated, down_rows, preferred_element_type=jnp.float32).astype(jnp.bfloat16)


def local(
    queries,
    span_keys,
    span_values,
    cache_keys,
    cache_values,
    lengths,
    inputs,
    w_out,
    norm_gain,
    route_ids,
    route_weights,
    w_gate_up,
    w_down,
):
    tok_rows = queries.shape[1]
    blk_count = lax.axis_size("blk")
    blk_index = lax.axis_index("blk")
    length = lengths[0]
    cache_len = cache_keys.shape[1]
    span_len = span_keys.shape[1]

    pairs = [(b, b ^ 1) for b in range(blk_count)]
    other_gate_up = lax.ppermute(w_gate_up[0], "blk", pairs)
    other_down = lax.ppermute(w_down[0], "blk", pairs)

    core = blk_index % 2
    half_cols = KV_HEADS * HEAD_DIM // 2
    key_rows = jnp.concatenate([cache_keys[0], span_keys[0]], 0)
    value_rows = jnp.concatenate([cache_values[0], span_values[0]], 0)

    def kv_cols(which):
        return jnp.concatenate(
            [
                lax.dynamic_slice_in_dim(key_rows, which * half_cols, half_cols, 1),
                lax.dynamic_slice_in_dim(value_rows, which * half_cols, half_cols, 1),
            ],
            1,
        )

    q_cols = queries.shape[2] // 2
    own_q = lax.dynamic_slice_in_dim(queries[0], core * q_cols, q_cols, 1)
    sent_q = lax.dynamic_slice_in_dim(queries[0], (1 - core) * q_cols, q_cols, 1)
    own_kv = kv_cols(core)
    got_kv, got_q = lax.ppermute((kv_cols(1 - core), sent_q), "blk", pairs)
    first = core == 0
    chip_kv = jnp.where(first, jnp.stack([own_kv, got_kv]), jnp.stack([got_kv, own_kv]))
    chip_q = jnp.where(first, jnp.concatenate([own_q, got_q], 0), jnp.concatenate([got_q, own_q], 0))
    same_core = [list(range(0, blk_count, 2)), list(range(1, blk_count, 2))]
    kv = lax.all_gather(chip_kv, "blk", axis=0, tiled=True, axis_index_groups=same_core)
    scalars = jnp.stack(
        [length, (blk_index - core).astype(jnp.int32), jnp.int32(cache_len)]
    )
    chip_out = attention(scalars, chip_q, kv, tok_rows)
    own_out = lax.dynamic_slice_in_dim(chip_out, core * tok_rows, tok_rows, 0)
    sent_out = lax.dynamic_slice_in_dim(chip_out, (1 - core) * tok_rows, tok_rows, 0)
    got_out = lax.ppermute(sent_out, "blk", pairs)
    attended = jnp.where(
        first, jnp.concatenate([own_out, got_out], 1), jnp.concatenate([got_out, own_out], 1)
    )
    attended, other_gate_up, other_down = lax.optimization_barrier(
        (attended, other_gate_up, other_down)
    )

    residual = inputs[0].astype(jnp.float32) + jnp.dot(
        attended, w_out, preferred_element_type=jnp.float32
    )
    normalized = (
        residual
        * lax.rsqrt(jnp.mean(residual * residual, axis=-1, keepdims=True) + 1e-06)
        * norm_gain
    ).astype(jnp.bfloat16)

    devices = lax.axis_size("req") * blk_count
    capacity = max(2, tok_rows * TOP * 2 // EXPERTS)
    half_cap = -(-((capacity + 1) // 2) // 8) * 8
    flat_ids = route_ids[0].reshape(-1)
    onehot = (flat_ids[:, None] == jnp.arange(EXPERTS, dtype=jnp.int32)[None, :]).astype(jnp.int32)
    slot_index = jnp.sum((jnp.cumsum(onehot, axis=0) - onehot) * onehot, axis=1)
    slot_target = (2 * flat_ids + slot_index % 2) * half_cap + slot_index // 2
    slot_match = slot_target[:, None] == jnp.arange(devices * half_cap, dtype=jnp.int32)[None, :]
    dispatch = jnp.sum(slot_match.reshape(tok_rows, TOP, -1).astype(jnp.float32), axis=1).astype(
        jnp.bfloat16
    )
    combine_weights = jnp.sum(
        jnp.where(slot_match, route_weights[0].reshape(-1)[:, None], 0.0).reshape(
            tok_rows, TOP, -1
        ),
        axis=1,
    )
    outgoing = lax.dot_general(
        dispatch, normalized, (((0,), (0,)), ((), ())), preferred_element_type=jnp.float32
    ).astype(jnp.bfloat16)
    arrived = lax.all_to_all(outgoing, ("req", "blk"), split_axis=0, concat_axis=0, tiled=True)
    mine = half_expert(arrived, w_gate_up[0], w_down[0])
    other = half_expert(arrived, other_gate_up, other_down)
    both = (mine.astype(jnp.float32) + other.astype(jnp.float32)).astype(jnp.bfloat16)
    returned = lax.all_to_all(both, ("req", "blk"), split_axis=0, concat_axis=0, tiled=True)
    weights_hi = combine_weights.astype(jnp.bfloat16)
    weights_lo = (combine_weights - weights_hi.astype(jnp.float32)).astype(jnp.bfloat16)
    expert_sum = jnp.dot(weights_hi, returned, preferred_element_type=jnp.float32) + jnp.dot(
        weights_lo, returned, preferred_element_type=jnp.float32
    )
    return (residual + expert_sum).astype(jnp.bfloat16)[None]


def solution(mesh):
    in_specs = (
        P("req", "blk", None),
        P("req", "blk", None),
        P("req", "blk", None),
        P("req", "blk", None),
        P("req", "blk", None),
        P("req"),
        P("req", "blk", None),
        P(),
        P(),
        P("req", "blk", None),
        P("req", "blk", None),
        P(("req", "blk"), None, None),
        P(("req", "blk"), None, None),
    )
    out_specs = P("req", "blk", None)
    return jax.shard_map(local, mesh=mesh, in_specs=in_specs, out_specs=out_specs, check_vma=False)
```

```python
import math

import jax
import jax.numpy as jnp
from jax import lax
from jax.experimental import pallas as pl
from jax.experimental.pallas import tpu as pltpu
from jax.sharding import PartitionSpec as P

D = 2048
HEADS = 16
KV_HEADS = 4
HEAD_DIM = 128
EXPERTS = 64
TOP = 6


CHUNK = 2048


def attn_kernel(s_ref, q_ref, k_ref, v_ref, o_ref):
    group_size = HEADS // KV_HEADS
    tok_rows = q_ref.shape[0]
    rows = tok_rows * group_size
    length = s_ref[0]
    blk = s_ref[1] + pl.program_id(1)
    qb = q_ref[...]
    qs = jnp.concatenate([qb[:, r * HEAD_DIM:(r + 1) * HEAD_DIM] for r in range(group_size)], axis=0)
    qpos = blk * tok_rows + lax.broadcasted_iota(jnp.int32, (rows, 1), 0) % tok_rows
    col = lax.broadcasted_iota(jnp.int32, (1, CHUNK), 1)
    cache_devs = CHUNK // CACHE_ROWS
    span_devs = CHUNK // SPAN_ROWS
    n_cache = (length + CHUNK - 1) // CHUNK
    n_span = (blk * tok_rows + tok_rows - 1) // CHUNK + 1
    factor = math.log2(math.e) / math.sqrt(HEAD_DIM)

    def cache_rows(ref, c):
        return ref[pl.ds(c * cache_devs, cache_devs), pl.ds(0, CACHE_ROWS), :].reshape(CHUNK, HEAD_DIM)

    def span_rows(ref, c):
        return ref[pl.ds(c * span_devs, span_devs), pl.ds(CACHE_ROWS, SPAN_ROWS), :].reshape(CHUNK, HEAD_DIM)

    def scores(k):
        return lax.dot_general(qs, k, (((1,), (1,)), ((), ())), preferred_element_type=jnp.float32)

    def cache_mask(c):
        return (c * CHUNK + col) < length

    def span_mask(c):
        return (c * CHUNK + col) <= qpos

    def step(rows_of, mask_of):
        def body(c, carry):
            m, l, acc = carry
            s = scores(rows_of(k_ref, c))
            if mask_of is not None:
                s = jnp.where(mask_of(c), s, -1e30)
            m_new = jnp.maximum(m, jnp.max(s, axis=-1, keepdims=True))
            alpha = jnp.exp2((m - m_new) * factor)
            p = jnp.exp2((s - m_new) * factor)
            l = alpha * l + jnp.sum(p, axis=-1, keepdims=True)
            acc = alpha * acc + jnp.dot(
                p.astype(jnp.bfloat16), rows_of(v_ref, c), preferred_element_type=jnp.float32
            )
            return m_new, l, acc
        return body

    carry = (
        jnp.full((rows, 1), -1e30, jnp.float32),
        jnp.zeros((rows, 1), jnp.float32),
        jnp.zeros((rows, HEAD_DIM), jnp.float32),
    )
    cache_full = length // CHUNK
    span_full = (blk * tok_rows + 1) // CHUNK
    carry = lax.fori_loop(0, cache_full, step(cache_rows, None), carry)
    carry = lax.fori_loop(cache_full, n_cache, step(cache_rows, cache_mask), carry)
    carry = lax.fori_loop(0, span_full, step(span_rows, None), carry)
    _, l, acc = lax.fori_loop(span_full, n_span, step(span_rows, span_mask), carry)
    out = (acc / l).astype(o_ref.dtype)
    for r in range(group_size):
        o_ref[:, r * HEAD_DIM:(r + 1) * HEAD_DIM] = out[r * tok_rows:(r + 1) * tok_rows]


CACHE_ROWS = 128
SPAN_ROWS = 64


def attention(scalars, queries, kv, tok_rows):
    groups = queries.shape[1] // (HEAD_DIM * HEADS // KV_HEADS)
    halves = queries.shape[0] // tok_rows
    devs, per_dev, _ = kv.shape
    group_cols = HEAD_DIM * HEADS // KV_HEADS
    return pl.pallas_call(
        attn_kernel,
        out_shape=jax.ShapeDtypeStruct(queries.shape, jnp.bfloat16),
        grid=(groups, halves),
        in_specs=[
            pl.BlockSpec(memory_space=pltpu.SMEM),
            pl.BlockSpec((tok_rows, group_cols), lambda g, h: (h, g)),
            pl.BlockSpec((devs, per_dev, HEAD_DIM), lambda g, h: (0, 0, g)),
            pl.BlockSpec((devs, per_dev, HEAD_DIM), lambda g, h: (0, 0, groups + g)),
        ],
        out_specs=pl.BlockSpec((tok_rows, group_cols), lambda g, h: (h, g)),
        compiler_params=pltpu.CompilerParams(
            dimension_semantics=("arbitrary", "arbitrary"), vmem_limit_bytes=40 * 1024 * 1024
        ),
    )(scalars, queries, kv, kv)


def half_expert(arrived, gate_up, down_rows):
    half_width = down_rows.shape[0]
    hidden = jnp.dot(arrived, gate_up.T, preferred_element_type=jnp.float32)
    activated = (jax.nn.silu(hidden[:, :half_width]) * hidden[:, half_width:]).astype(jnp.bfloat16)
    return jnp.dot(activated, down_rows, preferred_element_type=jnp.float32).astype(jnp.bfloat16)


def local(
    queries,
    span_keys,
    span_values,
    cache_keys,
    cache_values,
    lengths,
    inputs,
    w_out,
    norm_gain,
    route_ids,
    route_weights,
    w_gate_up,
    w_down,
):
    tok_rows = queries.shape[1]
    blk_count = lax.axis_size("blk")
    blk_index = lax.axis_index("blk")
    length = lengths[0]
    cache_len = cache_keys.shape[1]
    span_len = span_keys.shape[1]

    pairs = [(b, b ^ 1) for b in range(blk_count)]
    other_gate_up = lax.ppermute(w_gate_up[0], "blk", pairs)
    other_down = lax.ppermute(w_down[0], "blk", pairs)

    core = blk_index % 2
    half_cols = KV_HEADS * HEAD_DIM // 2
    key_rows = jnp.concatenate([cache_keys[0], span_keys[0]], 0)
    value_rows = jnp.concatenate([cache_values[0], span_values[0]], 0)

    def kv_cols(which):
        return jnp.concatenate(
            [
                lax.dynamic_slice_in_dim(key_rows, which * half_cols, half_cols, 1),
                lax.dynamic_slice_in_dim(value_rows, which * half_cols, half_cols, 1),
            ],
            1,
        )

    q_cols = queries.shape[2] // 2
    own_q = lax.dynamic_slice_in_dim(queries[0], core * q_cols, q_cols, 1)
    sent_q = lax.dynamic_slice_in_dim(queries[0], (1 - core) * q_cols, q_cols, 1)
    own_kv = kv_cols(core)
    got_kv, got_q = lax.ppermute((kv_cols(1 - core), sent_q), "blk", pairs)
    first = core == 0
    chip_kv = jnp.where(first, jnp.stack([own_kv, got_kv]), jnp.stack([got_kv, own_kv]))
    chip_q = jnp.where(first, jnp.concatenate([own_q, got_q], 0), jnp.concatenate([got_q, own_q], 0))
    same_core = [list(range(0, blk_count, 2)), list(range(1, blk_count, 2))]
    kv = lax.all_gather(chip_kv, "blk", axis=0, tiled=True, axis_index_groups=same_core)
    scalars = jnp.stack(
        [length, (blk_index - core).astype(jnp.int32), jnp.int32(cache_len)]
    )
    chip_out = attention(scalars, chip_q, kv, tok_rows)
    own_out = lax.dynamic_slice_in_dim(chip_out, core * tok_rows, tok_rows, 0)
    sent_out = lax.dynamic_slice_in_dim(chip_out, (1 - core) * tok_rows, tok_rows, 0)
    got_out = lax.ppermute(sent_out, "blk", pairs)
    attended = jnp.where(
        first, jnp.concatenate([own_out, got_out], 1), jnp.concatenate([got_out, own_out], 1)
    )
    attended, other_gate_up, other_down = lax.optimization_barrier(
        (attended, other_gate_up, other_down)
    )

    residual = inputs[0].astype(jnp.float32) + jnp.dot(
        attended, w_out, preferred_element_type=jnp.float32
    )
    normalized = (
        residual
        * lax.rsqrt(jnp.mean(residual * residual, axis=-1, keepdims=True) + 1e-06)
        * norm_gain
    ).astype(jnp.bfloat16)

    devices = lax.axis_size("req") * blk_count
    capacity = max(2, tok_rows * TOP * 2 // EXPERTS)
    half_cap = -(-((capacity + 1) // 2) // 8) * 8
    flat_ids = route_ids[0].reshape(-1)
    onehot = (flat_ids[:, None] == jnp.arange(EXPERTS, dtype=jnp.int32)[None, :]).astype(jnp.int32)
    slot_index = jnp.sum((jnp.cumsum(onehot, axis=0) - onehot) * onehot, axis=1)
    slot_target = (2 * flat_ids + slot_index % 2) * half_cap + slot_index // 2
    slot_match = slot_target[:, None] == jnp.arange(devices * half_cap, dtype=jnp.int32)[None, :]
    dispatch = jnp.sum(slot_match.reshape(tok_rows, TOP, -1).astype(jnp.float32), axis=1).astype(
        jnp.bfloat16
    )
    combine_weights = jnp.sum(
        jnp.where(slot_match, route_weights[0].reshape(-1)[:, None], 0.0).reshape(
            tok_rows, TOP, -1
        ),
        axis=1,
    )
    outgoing = lax.dot_general(
        dispatch, normalized, (((0,), (0,)), ((), ())), preferred_element_type=jnp.float32
    ).astype(jnp.bfloat16)
    arrived = lax.all_to_all(outgoing, ("req", "blk"), split_axis=0, concat_axis=0, tiled=True)
    mine = half_expert(arrived, w_gate_up[0], w_down[0])
    other = half_expert(arrived, other_gate_up, other_down)
    both = (mine.astype(jnp.float32) + other.astype(jnp.float32)).astype(jnp.bfloat16)
    returned = lax.all_to_all(both, ("req", "blk"), split_axis=0, concat_axis=0, tiled=True)
    expert_sum = jnp.dot(
        combine_weights,
        returned.astype(jnp.float32),
        precision=lax.Precision.HIGH,
        preferred_element_type=jnp.float32,
    )
    return (residual + expert_sum).astype(jnp.bfloat16)[None]


def solution(mesh):
    in_specs = (
        P("req", "blk", None),
        P("req", "blk", None),
        P("req", "blk", None),
        P("req", "blk", None),
        P("req", "blk", None),
        P("req"),
        P("req", "blk", None),
        P(),
        P(),
        P("req", "blk", None),
        P("req", "blk", None),
        P(("req", "blk"), None, None),
        P(("req", "blk"), None, None),
    )
    out_specs = P("req", "blk", None)
    return jax.shard_map(local, mesh=mesh, in_specs=in_specs, out_specs=out_specs, check_vma=False)
```
